32 devices in a mesh: dp: 4 (over y, x), expert: 8 (over z, core).
Axes of the slice: x: 2, y: 2, z: 4, core: 2. Of those that a mesh axis runs over, the one named last changes fastest.
Arguments:
- tokens: bfloat16 [4096, 4096], P(('dp', 'expert')), may hold values from -6 to 6
- expert_ids: int32 [4096, 2], P(('dp', 'expert')), may hold values from 0 to 7, all different within a row; in each aligned block of 128 rows (0 to 127, 128 to 255, ...) at most 64 rows name the same one
- combine: float32 [4096, 2], P(('dp', 'expert')), may hold values from 0.2 to 1
- weight_gate: bfloat16 [8, 768, 4096], P('expert'), may hold values from -0.09375 to 0.09375
- weight_up: bfloat16 [8, 768, 4096], P('expert'), may hold values from -0.09375 to 0.09375
- weight_down: bfloat16 [8, 768, 4096], P('expert'), may hold values from -0.21875 to 0.21875
- grad_out: bfloat16 [4096, 4096], P(('dp', 'expert')), may hold values from -6 to 6
Outputs:
- mixed: bfloat16 [4096, 4096], P(('dp', 'expert'))
- grad_tokens: bfloat16 [4096, 4096], P(('dp', 'expert'))
- grad_combine: float32 [4096, 2], P(('dp', 'expert'))
- grad_gate: bfloat16 [8, 768, 4096], P('expert', 'dp')
- grad_up: bfloat16 [8, 768, 4096], P('expert', 'dp')
- grad_down: bfloat16 [8, 768, 4096], P('expert', 'dp')
The draws below stay inside these ranges and needn't reach their ends.
Inputs may be any that keep to these rules, and one draw needn't show every extreme that they name: `expert_ids`: each row names 2 different experts. In the rows of one device no expert is named more than 64 times, a bound that some block reaches.
All inputs are finite; a program needn't handle non-finite values.
Results may differ from the reference program's by a relative error of at most 0.012.
Values may be sent and summed in bfloat16 or wider, within the bound.
No kernel may reach another device: no remote copies, remote signals or barrier semaphores. Data moves between devices by JAX's collectives and lax.ppermute only.
A program may use at most 192 MiB of HBM per device.

```python
import math
import jax
import jax.numpy as jnp
import numpy as np
from jax import lax

D = 4096
FF = 768
TOPK = 2
TOK_DEV = 128
E = 8
CAP = 64
TOKENS = 4096
N_DP = 4
N_EXPERT = 8


def block_levels(own_key, shape, shards, smallest, top_value):
    def one(axis_at, parts):
        draws = jax.random.uniform(jax.random.fold_in(jax.random.fold_in(own_key, 6), axis_at), (parts,), jnp.float32, smallest / len(shards), top_value / len(shards))
        return jnp.repeat(jnp.exp(draws), shape[axis_at] // parts).reshape((-1,) + (1,) * (len(shape) - axis_at - 1))

    loudness = one(*shards[0])
    for cut in shards[1:]:
        loudness = loudness * one(*cut)
    return loudness


def routed_block(rng, own, number, rows, amount, top, most, lean):
    sequence = jax.random.permutation(rng, amount)
    packed, ordinary = portions_of(amount, rows * top, most, lean, True), portions_of(amount, rows * top, most, lean, False)
    places = jnp.arange(amount)

    def named(lengths, turn):
        used = int((lengths > 0).sum())
        fixed = max(1, used // 4)
        moved = fixed + (places - fixed + turn * (used - fixed)) % max(1, amount - fixed)
        return jnp.zeros((amount,), jnp.int32).at[sequence[jnp.where(places < fixed, places, moved)]].set(jnp.asarray(lengths, jnp.int32))

    lengths = jnp.where(number % 4 == 0, named(packed, number // 4), named(ordinary, number - number // 4 - 1))
    mixed = jax.random.permutation(jax.random.fold_in(own, 3), amount)
    source_of, receiver = mixed[0:amount // 2 * 2:2], mixed[1:amount // 2 * 2:2]
    slack = jnp.minimum(lengths[source_of] - 1, most - lengths[receiver]) // 2
    slack = jnp.where((source_of == sequence[0]) | (receiver == sequence[0]) | (lengths[receiver] == 0), 0, jnp.maximum(slack, 0))
    moved = jax.random.randint(jax.random.fold_in(own, 4), (amount // 2,), 0, 1 << 20) % (slack + 1)
    lengths = lengths.at[source_of].add(-moved).at[receiver].add(moved)
    labels = jnp.searchsorted(jnp.cumsum(lengths), jnp.arange(rows * top), side="right").astype(jnp.int32)
    grid = labels.reshape(top, rows).T
    grid = grid[jax.random.permutation(jax.random.fold_in(own, 1), rows)]
    turn = jax.random.randint(jax.random.fold_in(own, 2), (rows, 1), 0, top)
    return jnp.take_along_axis(grid, (jnp.arange(top)[None, :] + turn) % top, axis=1)


def portions_of(count, total, most, slope, full):
    loads = [(1 << 20) // math.isqrt(standing ** slope) + 1 for standing in range(1, count + 1)]
    largest = most if full else min(most, max(-(-total // count), total * loads[0] // sum(loads)))
    least = 1 if total - largest >= count - 1 else 0
    holding, rest = [largest] + [least] * (count - 1), total - largest - least * (count - 1)
    while rest > 0:
        movable = [i for i in range(1, count) if holding[i] < largest] or [i for i in range(1, count) if holding[i] < most]
        whole, left = sum([loads[i] for i in movable]), rest
        for i in movable:
            addition = min(most - holding[i], max(1, left * loads[i] // whole), rest)
            holding[i] = holding[i] + addition
            rest = rest - addition
    return np.array(holding)


def bell_draw(key, extent, scale, reach, cuts=(), kind=jnp.bfloat16):
    loudness = block_levels(key, extent, cuts, -0.22, 0.18) if cuts else 1.0
    entries = jax.random.normal(key, extent, jnp.float32) * scale * loudness
    return jnp.minimum(jnp.maximum(entries, -reach), reach).astype(kind)


def setup_inputs(seed: int = 0) -> dict:
    key_list = jax.random.split(jax.random.key(seed), 8)
    tokens = bell_draw(key_list[0], (TOKENS, D), 1.0, 6.0, ((0, 32),))
    expert_ids_keys = jax.random.split(jax.random.fold_in(key_list[1], 1), TOKENS // TOK_DEV)
    expert_ids_turns = jax.random.permutation(jax.random.fold_in(key_list[1], 3), TOKENS // TOK_DEV)
    expert_ids = jax.vmap(lambda own, number: routed_block(jax.random.fold_in(key_list[1], 2), own, number, TOK_DEV, E, TOPK, CAP, 2))(expert_ids_keys, expert_ids_turns).reshape((TOKENS, TOPK))
    combine = jnp.clip(0.2 + 0.8 * jax.random.uniform(key_list[2], (TOKENS, TOPK), jnp.float32) ** block_levels(key_list[2], (TOKENS, TOPK), ((0, 32),), -0.2, 0.2), 0.2, 1.0)
    weight_gate = bell_draw(key_list[3], (E, FF, D), D ** -0.5, 0.09375, ((0, 8),))
    weight_up = bell_draw(key_list[4], (E, FF, D), D ** -0.5, 0.09375, ((0, 8),))
    weight_down = bell_draw(key_list[5], (E, FF, D), FF ** -0.5, 0.21875, ((0, 8),))
    grad_out = bell_draw(key_list[6], (TOKENS, D), 1.0, 6.0, ((0, 32),))
    return {"tokens": tokens, "expert_ids": expert_ids, "combine": combine, "weight_gate": weight_gate, "weight_up": weight_up, "weight_down": weight_down, "grad_out": grad_out}


def group_sum(left, right, scale):
    block_rows = N_EXPERT * CAP
    left_group = left.astype(jnp.float32).reshape(N_DP, block_rows, left.shape[1])
    right_group = right.astype(jnp.float32).reshape(N_DP, block_rows, right.shape[1])
    partial_sums = (scale * jnp.einsum("irf,ird->ifd", left_group, right_group, precision=lax.Precision.HIGHEST)).astype(jnp.bfloat16)
    return jnp.sum(partial_sums.astype(jnp.float32), axis=0).astype(jnp.bfloat16)


def reference(tokens, expert_ids, combine, weight_gate, weight_up, weight_down, grad_out):
    devices_all = N_DP * N_EXPERT
    pair_dev = TOK_DEV * TOPK
    pair_total = devices_all * pair_dev
    flat_ids = expert_ids.reshape(devices_all, pair_dev)
    onehot = (flat_ids[:, :, None] == jnp.arange(E, dtype=jnp.int32)[None, None, :]).astype(jnp.int32)
    earlier = jnp.cumsum(onehot, axis=1) - onehot
    position = jnp.sum(earlier * onehot, axis=2).astype(jnp.int32)
    device_ids = jnp.arange(devices_all, dtype=jnp.int32)[:, None]
    pair_ids = jnp.arange(pair_total, dtype=jnp.int32).reshape(devices_all, pair_dev)
    table = jnp.full((E, devices_all * CAP), pair_total, jnp.int32)
    table = table.at[flat_ids, device_ids * CAP + position].set(pair_ids)
    combine_flat = combine.reshape(pair_total)
    scale = (TOK_DEV * TOPK * N_DP) ** -0.5

    def expert_step(carry, inputs):
        out_acc, grad_acc, pair_acc = carry
        pair_row, w_gate, w_up, w_down = inputs
        valid = pair_row < pair_total
        pair_safe = jnp.minimum(pair_row, pair_total - 1)
        token_row = pair_safe // TOPK
        weight_pair = jnp.where(valid, combine_flat[pair_safe], jnp.zeros((), jnp.float32))
        in_rows = jnp.where(valid[:, None], tokens[token_row], jnp.zeros((), tokens.dtype))
        cotangent = grad_out[token_row].astype(jnp.float32)
        out_grads = (weight_pair[:, None] * cotangent).astype(jnp.bfloat16)
        gate_pre = jnp.dot(in_rows, w_gate.T, preferred_element_type=jnp.float32)
        up_pre = jnp.dot(in_rows, w_up.T, preferred_element_type=jnp.float32)
        sigmoid_gate = jax.nn.sigmoid(gate_pre)
        activated = (gate_pre * sigmoid_gate * up_pre).astype(jnp.bfloat16)
        expert_out = jnp.dot(activated, w_down, preferred_element_type=jnp.float32).astype(jnp.bfloat16)
        grad_act = jnp.dot(out_grads, w_down.T, preferred_element_type=jnp.float32)
        grad_gate_pre = (grad_act * up_pre * sigmoid_gate * (1.0 + gate_pre * (1.0 - sigmoid_gate))).astype(jnp.bfloat16)
        grad_up_pre = (grad_act * gate_pre * sigmoid_gate).astype(jnp.bfloat16)
        row_grads = (jnp.dot(grad_gate_pre, w_gate, preferred_element_type=jnp.float32)
                     + jnp.dot(grad_up_pre, w_up, preferred_element_type=jnp.float32)).astype(jnp.bfloat16)
        out_float = expert_out.astype(jnp.float32)
        out_acc = out_acc.at[token_row].add(weight_pair[:, None] * out_float)
        grad_acc = grad_acc.at[token_row].add(jnp.where(valid[:, None], row_grads.astype(jnp.float32), jnp.zeros((), jnp.float32)))
        pair_acc = pair_acc.at[pair_safe].add(jnp.where(valid, jnp.sum(cotangent * out_float, axis=1), jnp.zeros((), jnp.float32)))
        gate_grad = group_sum(grad_gate_pre, in_rows, scale)
        up_grad = group_sum(grad_up_pre, in_rows, scale)
        down_grad = group_sum(activated, out_grads, scale)
        return (out_acc, grad_acc, pair_acc), (gate_grad, up_grad, down_grad)

    start_state = (jnp.zeros((TOKENS, D), jnp.float32), jnp.zeros((TOKENS, D), jnp.float32), jnp.zeros((pair_total,), jnp.float32))
    final_state, grads = lax.scan(expert_step, start_state, (table, weight_gate, weight_up, weight_down))
    out_acc, grad_acc, pair_acc = final_state
    gate_grads, up_grads, down_grads = grads
    return (out_acc.astype(jnp.bfloat16), grad_acc.astype(jnp.bfloat16), pair_acc.reshape(TOKENS, TOPK),
            gate_grads, up_grads, down_grads)
```

```python
import jax
import jax.numpy as jnp
from jax import lax
from jax.sharding import PartitionSpec as P


def slot_targets(expert_ids, experts, capacity):
    tok_count, top_count = expert_ids.shape
    pair_total = tok_count * top_count
    flat_ids = expert_ids.reshape(pair_total)
    onehot = (flat_ids[:, None] == jnp.arange(experts, dtype=jnp.int32)[None, :]).astype(jnp.int32)
    earlier = jnp.cumsum(onehot, axis=0) - onehot
    position = jnp.sum(earlier * onehot, axis=1)
    return (flat_ids * capacity + position).reshape(tok_count, top_count)


def per_device(tokens, expert_ids, combine, weight_gate, weight_up, weight_down, grad_out):
    tok_count, top_count = expert_ids.shape
    model_width = tokens.shape[1]
    experts = lax.axis_size("expert")
    copies = lax.axis_size("dp")
    capacity = 2 * tok_count * top_count // experts
    slots = experts * capacity
    target = slot_targets(expert_ids, experts, capacity)
    slot_iota = jnp.arange(slots, dtype=jnp.int32)
    hit = target.T[:, :, None] == slot_iota[None, None, :]
    send_onehot = jnp.any(hit, axis=0).T.astype(jnp.bfloat16)
    weight_pair = jnp.sum(
        jnp.where(hit, combine.T[:, :, None], jnp.zeros((), jnp.float32)), axis=(0, 1)
    )
    with jax.named_scope("dispatch_rows"):
        send_rows = jnp.dot(send_onehot, tokens, preferred_element_type=jnp.float32).astype(
            jnp.bfloat16
        )
        send_go = jnp.dot(send_onehot, grad_out, preferred_element_type=jnp.float32)
        send_grads = (weight_pair[:, None] * send_go).astype(jnp.bfloat16)
    send_rows = send_rows.reshape(experts, capacity, model_width)
    send_grads = send_grads.reshape(experts, capacity, model_width)
    recv_rows = lax.all_to_all(send_rows, "expert", split_axis=0, concat_axis=0, tiled=True)
    recv_grads = lax.all_to_all(send_grads, "expert", split_axis=0, concat_axis=0, tiled=True)
    in_rows = recv_rows.reshape(slots, model_width)
    out_grads = recv_grads.reshape(slots, model_width)
    w_gate = weight_gate[0]
    w_up = weight_up[0]
    w_down = weight_down[0]
    gate_pre = jnp.dot(in_rows, w_gate.T, preferred_element_type=jnp.float32)
    up_pre = jnp.dot(in_rows, w_up.T, preferred_element_type=jnp.float32)
    sigmoid_gate = jax.nn.sigmoid(gate_pre)
    activated = (gate_pre * sigmoid_gate * up_pre).astype(jnp.bfloat16)
    expert_out = jnp.dot(activated, w_down, preferred_element_type=jnp.float32).astype(jnp.bfloat16)
    back_out = lax.all_to_all(
        expert_out.reshape(experts, capacity, model_width),
        "expert",
        split_axis=0,
        concat_axis=0,
        tiled=True,
    )
    scale = (tok_count * top_count * copies) ** (-0.5)
    grad_act = jnp.dot(out_grads, w_down.T, preferred_element_type=jnp.float32)
    grad_gate_pre = (
        grad_act * up_pre * sigmoid_gate * (1.0 + gate_pre * (1.0 - sigmoid_gate))
    ).astype(jnp.bfloat16)
    grad_up_pre = (grad_act * gate_pre * sigmoid_gate).astype(jnp.bfloat16)
    row_grads = (
        jnp.dot(grad_gate_pre, w_gate, preferred_element_type=jnp.float32)
        + jnp.dot(grad_up_pre, w_up, preferred_element_type=jnp.float32)
    ).astype(jnp.bfloat16)
    back_grads = lax.all_to_all(
        row_grads.reshape(experts, capacity, model_width),
        "expert",
        split_axis=0,
        concat_axis=0,
        tiled=True,
    )
    with jax.named_scope("weight_grads"):
        down_term = (
            scale * jnp.einsum("rf,rd->fd", activated, out_grads, preferred_element_type=jnp.float32)
        ).astype(jnp.bfloat16)
        gate_term = (
            scale * jnp.einsum("rf,rd->fd", grad_gate_pre, in_rows, preferred_element_type=jnp.float32)
        ).astype(jnp.bfloat16)
        up_term = (
            scale * jnp.einsum("rf,rd->fd", grad_up_pre, in_rows, preferred_element_type=jnp.float32)
        ).astype(jnp.bfloat16)
    down_share = lax.psum_scatter(down_term, "dp", scatter_dimension=0, tiled=True)
    gate_share = lax.psum_scatter(gate_term, "dp", scatter_dimension=0, tiled=True)
    up_share = lax.psum_scatter(up_term, "dp", scatter_dimension=0, tiled=True)
    pick_onehot = hit.reshape(top_count * tok_count, slots).astype(jnp.bfloat16)
    with jax.named_scope("combine_rows"):
        picked_out = jnp.dot(
            pick_onehot, back_out.reshape(slots, model_width), preferred_element_type=jnp.float32
        ).reshape(top_count, tok_count, model_width)
        grad_f32 = grad_out.astype(jnp.float32)
        mixed = combine[:, 0:1] * picked_out[0]
        for k in range(1, top_count):
            mixed = mixed + combine[:, k : k + 1] * picked_out[k]
        mixed = mixed.astype(jnp.bfloat16)
        grad_combine = jnp.stack(
            [jnp.sum(grad_f32 * picked_out[k], axis=1) for k in range(top_count)], axis=1
        )
        picked_grads = jnp.dot(
            pick_onehot, back_grads.reshape(slots, model_width), preferred_element_type=jnp.float32
        ).reshape(top_count, tok_count, model_width)
        grad_tokens = picked_grads[0]
        for k in range(1, top_count):
            grad_tokens = grad_tokens + picked_grads[k]
        grad_tokens = grad_tokens.astype(jnp.bfloat16)
    return (mixed, grad_tokens, grad_combine, gate_share[None], up_share[None], down_share[None])


def solution(mesh):
    in_specs = (
        P(("dp", "expert"), None),
        P(("dp", "expert"), None),
        P(("dp", "expert"), None),
        P("expert", None, None),
        P("expert", None, None),
        P("expert", None, None),
        P(("dp", "expert"), None),
    )
    out_specs = (
        P(("dp", "expert"), None),
        P(("dp", "expert"), None),
        P(("dp", "expert"), None),
        P("expert", "dp", None),
        P("expert", "dp", None),
        P("expert", "dp", None),
    )
    return jax.shard_map(
        per_device, mesh=mesh, in_specs=in_specs, out_specs=out_specs, check_vma=False
    )
```

```python
import jax
import jax.numpy as jnp
from jax import lax
from jax.sharding import PartitionSpec as P


def slot_targets(expert_ids, experts, capacity):
    tok_count, top_count = expert_ids.shape
    pair_total = tok_count * top_count
    flat_ids = expert_ids.reshape(pair_total)
    onehot = (flat_ids[:, None] == jnp.arange(experts, dtype=jnp.int32)[None, :]).astype(jnp.int32)
    earlier = jnp.cumsum(onehot, axis=0) - onehot
    position = jnp.sum(earlier * onehot, axis=1)
    return (flat_ids * capacity + position).reshape(tok_count, top_count)


def per_device(tokens, expert_ids, combine, weight_gate, weight_up, weight_down, grad_out):
    tok_count, top_count = expert_ids.shape
    model_width = tokens.shape[1]
    experts = lax.axis_size("expert")
    copies = lax.axis_size("dp")
    capacity = 2 * tok_count * top_count // experts
    slots = experts * capacity
    target = slot_targets(expert_ids, experts, capacity)
    slot_iota = jnp.arange(slots, dtype=jnp.int32)
    hit = target.T[:, :, None] == slot_iota[None, None, :]
    send_onehot = jnp.any(hit, axis=0).T.astype(jnp.bfloat16)
    weight_pair = jnp.sum(
        jnp.where(hit, combine.T[:, :, None], jnp.zeros((), jnp.float32)), axis=(0, 1)
    )
    with jax.named_scope("dispatch_rows"):
        send_rows = jnp.dot(send_onehot, tokens, preferred_element_type=jnp.float32).astype(
            jnp.bfloat16
        )
        send_go = jnp.dot(send_onehot, grad_out, preferred_element_type=jnp.float32)
        send_grads = (weight_pair[:, None] * send_go).astype(jnp.bfloat16)
    send_rows = send_rows.reshape(experts, capacity, model_width)
    send_grads = send_grads.reshape(experts, capacity, model_width)
    recv_rows = lax.all_to_all(send_rows, "expert", split_axis=0, concat_axis=0, tiled=True)
    recv_rows, send_grads = lax.optimization_barrier((recv_rows, send_grads))
    recv_grads = lax.all_to_all(send_grads, "expert", split_axis=0, concat_axis=0, tiled=True)
    in_rows = recv_rows.reshape(slots, model_width)
    out_grads = recv_grads.reshape(slots, model_width)
    w_gate = weight_gate[0]
    w_up = weight_up[0]
    w_down = weight_down[0]
    def forward(rows):
        gate_pre = jnp.dot(rows, w_gate.T, preferred_element_type=jnp.float32)
        up_pre = jnp.dot(rows, w_up.T, preferred_element_type=jnp.float32)
        sigmoid_gate = jax.nn.sigmoid(gate_pre)
        activated = (gate_pre * sigmoid_gate * up_pre).astype(jnp.bfloat16)
        expert_out = jnp.dot(activated, w_down, preferred_element_type=jnp.float32).astype(
            jnp.bfloat16
        )
        return gate_pre, up_pre, sigmoid_gate, activated, expert_out

    always = expert_ids[0, 0] >= 0
    gate_pre, up_pre, sigmoid_gate, activated, expert_out = lax.cond(
        always, forward, forward, in_rows
    )
    back_out = lax.all_to_all(
        expert_out.reshape(experts, capacity, model_width),
        "expert",
        split_axis=0,
        concat_axis=0,
        tiled=True,
    )
    scale = (tok_count * top_count * copies) ** (-0.5)
    grad_act = jnp.dot(out_grads, w_down.T, preferred_element_type=jnp.float32)
    grad_gate_pre = (
        grad_act * up_pre * sigmoid_gate * (1.0 + gate_pre * (1.0 - sigmoid_gate))
    ).astype(jnp.bfloat16)
    grad_up_pre = (grad_act * gate_pre * sigmoid_gate).astype(jnp.bfloat16)
    row_grads = (
        jnp.dot(grad_gate_pre, w_gate, preferred_element_type=jnp.float32)
        + jnp.dot(grad_up_pre, w_up, preferred_element_type=jnp.float32)
    ).astype(jnp.bfloat16)
    back_grads = lax.all_to_all(
        row_grads.reshape(experts, capacity, model_width),
        "expert",
        split_axis=0,
        concat_axis=0,
        tiled=True,
    )
    with jax.named_scope("weight_grads"):
        down_term = (
            scale * jnp.einsum("rf,rd->fd", activated, out_grads, preferred_element_type=jnp.float32)
        ).astype(jnp.bfloat16)
        gate_term = (
            scale * jnp.einsum("rf,rd->fd", grad_gate_pre, in_rows, preferred_element_type=jnp.float32)
        ).astype(jnp.bfloat16)
        up_term = (
            scale * jnp.einsum("rf,rd->fd", grad_up_pre, in_rows, preferred_element_type=jnp.float32)
        ).astype(jnp.bfloat16)
    down_share = lax.psum_scatter(down_term, "dp", scatter_dimension=0, tiled=True)
    gate_share = lax.psum_scatter(gate_term, "dp", scatter_dimension=0, tiled=True)
    up_share = lax.psum_scatter(up_term, "dp", scatter_dimension=0, tiled=True)
    pick_onehot = hit.reshape(top_count * tok_count, slots).astype(jnp.bfloat16)
    with jax.named_scope("combine_rows"):
        picked_out = jnp.dot(
            pick_onehot, back_out.reshape(slots, model_width), preferred_element_type=jnp.float32
        ).reshape(top_count, tok_count, model_width)
        grad_f32 = grad_out.astype(jnp.float32)
        mixed = combine[:, 0:1] * picked_out[0]
        for k in range(1, top_count):
            mixed = mixed + combine[:, k : k + 1] * picked_out[k]
        mixed = mixed.astype(jnp.bfloat16)
        grad_combine = jnp.stack(
            [jnp.sum(grad_f32 * picked_out[k], axis=1) for k in range(top_count)], axis=1
        )
        picked_grads = jnp.dot(
            pick_onehot, back_grads.reshape(slots, model_width), preferred_element_type=jnp.float32
        ).reshape(top_count, tok_count, model_width)
        grad_tokens = picked_grads[0]
        for k in range(1, top_count):
            grad_tokens = grad_tokens + picked_grads[k]
        grad_tokens = grad_tokens.astype(jnp.bfloat16)
    return (mixed, grad_tokens, grad_combine, gate_share[None], up_share[None], down_share[None])


def solution(mesh):
    in_specs = (
        P(("dp", "expert"), None),
        P(("dp", "expert"), None),
        P(("dp", "expert"), None),
        P("expert", None, None),
        P("expert", None, None),
        P("expert", None, None),
        P(("dp", "expert"), None),
    )
    out_specs = (
        P(("dp", "expert"), None),
        P(("dp", "expert"), None),
        P(("dp", "expert"), None),
        P("expert", "dp", None),
        P("expert", "dp", None),
        P("expert", "dp", None),
    )
    return jax.shard_map(
        per_device, mesh=mesh, in_specs=in_specs, out_specs=out_specs, check_vma=False
    )
```

```python
import jax
import jax.numpy as jnp
from jax import lax
from jax.sharding import PartitionSpec as P


def slot_targets(expert_ids, experts, capacity):
    tok_count, top_count = expert_ids.shape
    pair_total = tok_count * top_count
    flat_ids = expert_ids.reshape(pair_total)
    onehot = (flat_ids[:, None] == jnp.arange(experts, dtype=jnp.int32)[None, :]).astype(jnp.int32)
    earlier = jnp.cumsum(onehot, axis=0) - onehot
    position = jnp.sum(earlier * onehot, axis=1)
    return (flat_ids * capacity + position).reshape(tok_count, top_count)


def per_device(tokens, expert_ids, combine, weight_gate, weight_up, weight_down, grad_out):
    tok_count, top_count = expert_ids.shape
    model_width = tokens.shape[1]
    experts = lax.axis_size("expert")
    copies = lax.axis_size("dp")
    capacity = 2 * tok_count * top_count // experts
    slots = experts * capacity
    target = slot_targets(expert_ids, experts, capacity)
    slot_iota = jnp.arange(slots, dtype=jnp.int32)
    hit = target.T[:, :, None] == slot_iota[None, None, :]
    send_onehot = jnp.any(hit, axis=0).T.astype(jnp.bfloat16)
    weight_pair = jnp.sum(
        jnp.where(hit, combine.T[:, :, None], jnp.zeros((), jnp.float32)), axis=(0, 1)
    )
    with jax.named_scope("dispatch_rows"):
        send_rows = jnp.dot(send_onehot, tokens, preferred_element_type=jnp.float32).astype(
            jnp.bfloat16
        )
        send_go = jnp.dot(send_onehot, grad_out, preferred_element_type=jnp.float32)
        send_grads = (weight_pair[:, None] * send_go).astype(jnp.bfloat16)
    send_rows = send_rows.reshape(experts, capacity, model_width)
    send_grads = send_grads.reshape(experts, capacity, model_width)
    recv_rows = lax.all_to_all(send_rows, "expert", split_axis=0, concat_axis=0, tiled=True)
    recv_rows, send_grads = lax.optimization_barrier((recv_rows, send_grads))
    recv_grads = lax.all_to_all(send_grads, "expert", split_axis=0, concat_axis=0, tiled=True)
    in_rows = recv_rows.reshape(slots, model_width)
    out_grads = recv_grads.reshape(slots, model_width)
    w_gate = weight_gate[0]
    w_up = weight_up[0]
    w_down = weight_down[0]
    def forward(rows):
        gate_pre = jnp.dot(rows, w_gate.T, preferred_element_type=jnp.float32)
        up_pre = jnp.dot(rows, w_up.T, preferred_element_type=jnp.float32)
        sigmoid_gate = jax.nn.sigmoid(gate_pre)
        activated = (gate_pre * sigmoid_gate * up_pre).astype(jnp.bfloat16)
        expert_out = jnp.dot(activated, w_down, preferred_element_type=jnp.float32).astype(
            jnp.bfloat16
        )
        return gate_pre, up_pre, sigmoid_gate, activated, expert_out

    always = expert_ids[0, 0] >= 0
    gate_pre, up_pre, sigmoid_gate, activated, expert_out = lax.cond(
        always, forward, forward, in_rows
    )
    back_out = lax.all_to_all(
        expert_out.reshape(experts, capacity, model_width),
        "expert",
        split_axis=0,
        concat_axis=0,
        tiled=True,
    )
    scale = (tok_count * top_count * copies) ** (-0.5)
    grad_act = jnp.dot(out_grads, w_down.T, preferred_element_type=jnp.float32)
    grad_gate_pre = (
        grad_act * up_pre * sigmoid_gate * (1.0 + gate_pre * (1.0 - sigmoid_gate))
    ).astype(jnp.bfloat16)
    grad_up_pre = (grad_act * gate_pre * sigmoid_gate).astype(jnp.bfloat16)
    row_grads = (
        jnp.dot(grad_gate_pre, w_gate, preferred_element_type=jnp.float32)
        + jnp.dot(grad_up_pre, w_up, preferred_element_type=jnp.float32)
    ).astype(jnp.bfloat16)
    back_grads = lax.all_to_all(
        row_grads.reshape(experts, capacity, model_width),
        "expert",
        split_axis=0,
        concat_axis=0,
        tiled=True,
    )
    ff_share = w_gate.shape[0] // copies
    with jax.named_scope("weight_grads"):
        down_term = (
            scale * jnp.einsum("rf,rd->fd", activated, out_grads, preferred_element_type=jnp.float32)
        ).astype(jnp.bfloat16)
        gate_up_pre = jnp.stack(
            [
                grad_gate_pre.reshape(slots, copies, ff_share),
                grad_up_pre.reshape(slots, copies, ff_share),
            ],
            axis=2,
        ).reshape(slots, copies * 2 * ff_share)
        gate_up_term = (
            scale * jnp.einsum("rf,rd->fd", gate_up_pre, in_rows, preferred_element_type=jnp.float32)
        ).astype(jnp.bfloat16)
    down_share = lax.psum_scatter(down_term, "dp", scatter_dimension=0, tiled=True)
    gate_up_share = lax.psum_scatter(gate_up_term, "dp", scatter_dimension=0, tiled=True)
    gate_share = gate_up_share[:ff_share]
    up_share = gate_up_share[ff_share:]
    pick_onehot = hit.reshape(top_count * tok_count, slots).astype(jnp.bfloat16)
    with jax.named_scope("combine_rows"):
        picked_out = jnp.dot(
            pick_onehot, back_out.reshape(slots, model_width), preferred_element_type=jnp.float32
        ).reshape(top_count, tok_count, model_width)
        grad_f32 = grad_out.astype(jnp.float32)
        mixed = combine[:, 0:1] * picked_out[0]
        for k in range(1, top_count):
            mixed = mixed + combine[:, k : k + 1] * picked_out[k]
        mixed = mixed.astype(jnp.bfloat16)
        grad_combine = jnp.stack(
            [jnp.sum(grad_f32 * picked_out[k], axis=1) for k in range(top_count)], axis=1
        )
        picked_grads = jnp.dot(
            pick_onehot, back_grads.reshape(slots, model_width), preferred_element_type=jnp.float32
        ).reshape(top_count, tok_count, model_width)
        grad_tokens = picked_grads[0]
        for k in range(1, top_count):
            grad_tokens = grad_tokens + picked_grads[k]
        grad_tokens = grad_tokens.astype(jnp.bfloat16)
    return (mixed, grad_tokens, grad_combine, gate_share[None], up_share[None], down_share[None])


def solution(mesh):
    in_specs = (
        P(("dp", "expert"), None),
        P(("dp", "expert"), None),
        P(("dp", "expert"), None),
        P("expert", None, None),
        P("expert", None, None),
        P("expert", None, None),
        P(("dp", "expert"), None),
    )
    out_specs = (
        P(("dp", "expert"), None),
        P(("dp", "expert"), None),
        P(("dp", "expert"), None),
        P("expert", "dp", None),
        P("expert", "dp", None),
        P("expert", "dp", None),
    )
    return jax.shard_map(
        per_device, mesh=mesh, in_specs=in_specs, out_specs=out_specs, check_vma=False
    )
```

```python
import jax
import jax.numpy as jnp
from jax import lax
from jax.sharding import PartitionSpec as P


def slot_targets(expert_ids, experts, capacity):
    tok_count, top_count = expert_ids.shape
    pair_total = tok_count * top_count
    flat_ids = expert_ids.reshape(pair_total)
    onehot = (flat_ids[:, None] == jnp.arange(experts, dtype=jnp.int32)[None, :]).astype(jnp.int32)
    earlier = jnp.cumsum(onehot, axis=0) - onehot
    position = jnp.sum(earlier * onehot, axis=1)
    return (flat_ids * capacity + position).reshape(tok_count, top_count)


def per_device(tokens, expert_ids, combine, weight_gate, weight_up, weight_down, grad_out):
    tok_count, top_count = expert_ids.shape
    model_width = tokens.shape[1]
    experts = lax.axis_size("expert")
    copies = lax.axis_size("dp")
    capacity = 2 * tok_count * top_count // experts
    slots = experts * capacity
    target = slot_targets(expert_ids, experts, capacity)
    slot_iota = jnp.arange(slots, dtype=jnp.int32)
    hit = target.T[:, :, None] == slot_iota[None, None, :]
    send_onehot = jnp.any(hit, axis=0).T.astype(jnp.bfloat16)
    weight_pair = jnp.sum(
        jnp.where(hit, combine.T[:, :, None], jnp.zeros((), jnp.float32)), axis=(0, 1)
    )
    with jax.named_scope("dispatch_rows"):
        send_rows = jnp.dot(send_onehot, tokens, preferred_element_type=jnp.float32).astype(
            jnp.bfloat16
        )
        send_go = jnp.dot(send_onehot, grad_out, preferred_element_type=jnp.float32)
        send_grads = (weight_pair[:, None] * send_go).astype(jnp.bfloat16)
    send_rows = send_rows.reshape(experts, capacity, model_width)
    send_grads = send_grads.reshape(experts, capacity, model_width)
    recv_rows = lax.all_to_all(send_rows, "expert", split_axis=0, concat_axis=0, tiled=True)
    recv_rows, send_grads = lax.optimization_barrier((recv_rows, send_grads))
    recv_grads = lax.all_to_all(send_grads, "expert", split_axis=0, concat_axis=0, tiled=True)
    in_rows = recv_rows.reshape(slots, model_width)
    out_grads = recv_grads.reshape(slots, model_width)
    w_gate = weight_gate[0]
    w_up = weight_up[0]
    w_down = weight_down[0]
    def forward(rows):
        gate_pre = jnp.dot(rows, w_gate.T, preferred_element_type=jnp.float32)
        up_pre = jnp.dot(rows, w_up.T, preferred_element_type=jnp.float32)
        sigmoid_gate = jax.nn.sigmoid(gate_pre)
        activated = (gate_pre * sigmoid_gate * up_pre).astype(jnp.bfloat16)
        expert_out = jnp.dot(activated, w_down, preferred_element_type=jnp.float32).astype(
            jnp.bfloat16
        )
        return gate_pre, up_pre, sigmoid_gate, activated, expert_out

    always = expert_ids[0, 0] >= 0
    gate_pre, up_pre, sigmoid_gate, activated, expert_out = lax.cond(
        always, forward, forward, in_rows
    )
    back_out = lax.all_to_all(
        expert_out.reshape(experts, capacity, model_width),
        "expert",
        split_axis=0,
        concat_axis=0,
        tiled=True,
    )
    scale = (tok_count * top_count * copies) ** (-0.5)
    grad_act = jnp.dot(out_grads, w_down.T, preferred_element_type=jnp.float32)
    grad_gate_pre = (
        grad_act * up_pre * sigmoid_gate * (1.0 + gate_pre * (1.0 - sigmoid_gate))
    ).astype(jnp.bfloat16)
    grad_up_pre = (grad_act * gate_pre * sigmoid_gate).astype(jnp.bfloat16)
    row_grads = (
        jnp.dot(grad_gate_pre, w_gate, preferred_element_type=jnp.float32)
        + jnp.dot(grad_up_pre, w_up, preferred_element_type=jnp.float32)
    ).astype(jnp.bfloat16)
    back_grads = lax.all_to_all(
        row_grads.reshape(experts, capacity, model_width),
        "expert",
        split_axis=0,
        concat_axis=0,
        tiled=True,
    )
    ff_share = w_gate.shape[0] // copies
    with jax.named_scope("weight_grads"):
        down_term = (
            scale * jnp.einsum("rf,rd->fd", activated, out_grads, preferred_element_type=jnp.float32)
        ).astype(jnp.bfloat16)
        gate_up_pre = jnp.stack(
            [
                grad_gate_pre.reshape(slots, copies, ff_share),
                grad_up_pre.reshape(slots, copies, ff_share),
            ],
            axis=2,
        ).reshape(slots, copies * 2 * ff_share)
        gate_up_term = (
            scale * jnp.einsum("rf,rd->fd", gate_up_pre, in_rows, preferred_element_type=jnp.float32)
        ).astype(jnp.bfloat16)
    down_share = lax.psum_scatter(down_term, "dp", scatter_dimension=0, tiled=True)
    gate_up_share = lax.psum_scatter(gate_up_term, "dp", scatter_dimension=0, tiled=True)
    gate_share = gate_up_share[:ff_share]
    up_share = gate_up_share[ff_share:]
    back_grads, gate_share, up_share, down_share = lax.optimization_barrier(
        (back_grads, gate_share, up_share, down_share)
    )
    pick_onehot = hit.reshape(top_count * tok_count, slots).astype(jnp.bfloat16)
    with jax.named_scope("combine_rows"):
        picked_out = jnp.dot(
            pick_onehot, back_out.reshape(slots, model_width), preferred_element_type=jnp.float32
        ).reshape(top_count, tok_count, model_width)
        grad_f32 = grad_out.astype(jnp.float32)
        mixed = combine[:, 0:1] * picked_out[0]
        for k in range(1, top_count):
            mixed = mixed + combine[:, k : k + 1] * picked_out[k]
        mixed = mixed.astype(jnp.bfloat16)
        grad_combine = jnp.stack(
            [jnp.sum(grad_f32 * picked_out[k], axis=1) for k in range(top_count)], axis=1
        )
        picked_grads = jnp.dot(
            pick_onehot, back_grads.reshape(slots, model_width), preferred_element_type=jnp.float32
        ).reshape(top_count, tok_count, model_width)
        grad_tokens = picked_grads[0]
        for k in range(1, top_count):
            grad_tokens = grad_tokens + picked_grads[k]
        grad_tokens = grad_tokens.astype(jnp.bfloat16)
    return (mixed, grad_tokens, grad_combine, gate_share[None], up_share[None], down_share[None])


def solution(mesh):
    in_specs = (
        P(("dp", "expert"), None),
        P(("dp", "expert"), None),
        P(("dp", "expert"), None),
        P("expert", None, None),
        P("expert", None, None),
        P("expert", None, None),
        P(("dp", "expert"), None),
    )
    out_specs = (
        P(("dp", "expert"), None),
        P(("dp", "expert"), None),
        P(("dp", "expert"), None),
        P("expert", "dp", None),
        P("expert", "dp", None),
        P("expert", "dp", None),
    )
    return jax.shard_map(
        per_device, mesh=mesh, in_specs=in_specs, out_specs=out_specs, check_vma=False
    )
```

```python
import jax
import jax.numpy as jnp
from jax import lax
from jax.sharding import PartitionSpec as P


def slot_targets(expert_ids, experts, capacity):
    tok_count, top_count = expert_ids.shape
    pair_total = tok_count * top_count
    flat_ids = expert_ids.reshape(pair_total)
    onehot = (flat_ids[:, None] == jnp.arange(experts, dtype=jnp.int32)[None, :]).astype(jnp.int32)
    earlier = jnp.cumsum(onehot, axis=0) - onehot
    position = jnp.sum(earlier * onehot, axis=1)
    return (flat_ids * capacity + position).reshape(tok_count, top_count)


def per_device(tokens, expert_ids, combine, weight_gate, weight_up, weight_down, grad_out):
    tok_count, top_count = expert_ids.shape
    model_width = tokens.shape[1]
    experts = lax.axis_size("expert")
    copies = lax.axis_size("dp")
    capacity = 2 * tok_count * top_count // experts
    slots = experts * capacity
    target = slot_targets(expert_ids, experts, capacity)
    slot_iota = jnp.arange(slots, dtype=jnp.int32)
    hit = target.T[:, :, None] == slot_iota[None, None, :]
    send_onehot = jnp.any(hit, axis=0).T.astype(jnp.bfloat16)
    weight_pair = jnp.sum(
        jnp.where(hit, combine.T[:, :, None], jnp.zeros((), jnp.float32)), axis=(0, 1)
    )
    with jax.named_scope("dispatch_rows"):
        send_rows = jnp.dot(send_onehot, tokens, preferred_element_type=jnp.float32).astype(
            jnp.bfloat16
        )
        send_go = jnp.dot(send_onehot, grad_out, preferred_element_type=jnp.float32)
        send_grads = (weight_pair[:, None] * send_go).astype(jnp.bfloat16)
    send_rows = send_rows.reshape(experts, capacity, model_width)
    send_grads = send_grads.reshape(experts, capacity, model_width)
    recv_rows = lax.all_to_all(send_rows, "expert", split_axis=0, concat_axis=0, tiled=True)
    recv_rows, send_grads = lax.optimization_barrier((recv_rows, send_grads))
    recv_grads = lax.all_to_all(send_grads, "expert", split_axis=0, concat_axis=0, tiled=True)
    in_rows = recv_rows.reshape(slots, model_width)
    out_grads = recv_grads.reshape(slots, model_width)
    w_gate = weight_gate[0]
    w_up = weight_up[0]
    w_down = weight_down[0]
    def forward(rows):
        gate_pre = jnp.dot(rows, w_gate.T, preferred_element_type=jnp.float32)
        up_pre = jnp.dot(rows, w_up.T, preferred_element_type=jnp.float32)
        sigmoid_gate = jax.nn.sigmoid(gate_pre)
        activated = (gate_pre * sigmoid_gate * up_pre).astype(jnp.bfloat16)
        expert_out = jnp.dot(activated, w_down, preferred_element_type=jnp.float32).astype(
            jnp.bfloat16
        )
        return gate_pre, up_pre, sigmoid_gate, activated, expert_out

    always = expert_ids[0, 0] >= 0
    gate_pre, up_pre, sigmoid_gate, activated, expert_out = lax.cond(
        always, forward, forward, in_rows
    )
    back_out = lax.all_to_all(
        expert_out.reshape(experts, capacity, model_width),
        "expert",
        split_axis=0,
        concat_axis=0,
        tiled=True,
    )
    scale = (tok_count * top_count * copies) ** (-0.5)
    grad_act = jnp.dot(out_grads, w_down.T, preferred_element_type=jnp.float32)
    grad_gate_pre = (
        grad_act * up_pre * sigmoid_gate * (1.0 + gate_pre * (1.0 - sigmoid_gate))
    ).astype(jnp.bfloat16)
    grad_up_pre = (grad_act * gate_pre * sigmoid_gate).astype(jnp.bfloat16)
    row_grads = (
        jnp.dot(grad_gate_pre, w_gate, preferred_element_type=jnp.float32)
        + jnp.dot(grad_up_pre, w_up, preferred_element_type=jnp.float32)
    ).astype(jnp.bfloat16)
    back_grads = lax.all_to_all(
        row_grads.reshape(experts, capacity, model_width),
        "expert",
        split_axis=0,
        concat_axis=0,
        tiled=True,
    )
    ff_share = w_gate.shape[0] // copies
    with jax.named_scope("weight_grads"):
        down_term = (
            scale * jnp.einsum("rf,rd->fd", activated, out_grads, preferred_element_type=jnp.float32)
        ).astype(jnp.bfloat16)
        gate_up_pre = jnp.stack(
            [
                grad_gate_pre.reshape(slots, copies, ff_share),
                grad_up_pre.reshape(slots, copies, ff_share),
            ],
            axis=2,
        ).reshape(slots, copies * 2 * ff_share)
        gate_up_term = (
            scale * jnp.einsum("rf,rd->fd", gate_up_pre, in_rows, preferred_element_type=jnp.float32)
        ).astype(jnp.bfloat16)
    down_share = lax.psum_scatter(down_term, "dp", scatter_dimension=0, tiled=True)
    gate_up_share = lax.psum_scatter(gate_up_term, "dp", scatter_dimension=0, tiled=True)
    gate_share = gate_up_share[:ff_share]
    up_share = gate_up_share[ff_share:]
    pick_onehot = hit.reshape(top_count * tok_count, slots).astype(jnp.bfloat16)
    with jax.named_scope("combine_rows"):
        picked_out = jnp.dot(
            pick_onehot, back_out.reshape(slots, model_width), preferred_element_type=jnp.float32
        ).reshape(top_count, tok_count, model_width)
        grad_f32 = grad_out.astype(jnp.float32)
        mixed = combine[:, 0:1] * picked_out[0]
        for k in range(1, top_count):
            mixed = mixed + combine[:, k : k + 1] * picked_out[k]
        mixed = mixed.astype(jnp.bfloat16)
        grad_combine = jnp.stack(
            [jnp.sum(grad_f32 * picked_out[k], axis=1) for k in range(top_count)], axis=1
        )
        back_grads, gate_share, up_share, mixed, grad_combine = lax.optimization_barrier(
            (back_grads, gate_share, up_share, mixed, grad_combine)
        )
        picked_grads = jnp.dot(
            pick_onehot, back_grads.reshape(slots, model_width), preferred_element_type=jnp.float32
        ).reshape(top_count, tok_count, model_width)
        grad_tokens = picked_grads[0]
        for k in range(1, top_count):
            grad_tokens = grad_tokens + picked_grads[k]
        grad_tokens = grad_tokens.astype(jnp.bfloat16)
    return (mixed, grad_tokens, grad_combine, gate_share[None], up_share[None], down_share[None])


def solution(mesh):
    in_specs = (
        P(("dp", "expert"), None),
        P(("dp", "expert"), None),
        P(("dp", "expert"), None),
        P("expert", None, None),
        P("expert", None, None),
        P("expert", None, None),
        P(("dp", "expert"), None),
    )
    out_specs = (
        P(("dp", "expert"), None),
        P(("dp", "expert"), None),
        P(("dp", "expert"), None),
        P("expert", "dp", None),
        P("expert", "dp", None),
        P("expert", "dp", None),
    )
    return jax.shard_map(
        per_device, mesh=mesh, in_specs=in_specs, out_specs=out_specs, check_vma=False
    )
```

```python
import jax
import jax.numpy as jnp
from jax import lax
from jax.sharding import PartitionSpec as P


def slot_targets(expert_ids, experts, capacity):
    tok_count, top_count = expert_ids.shape
    pair_total = tok_count * top_count
    flat_ids = expert_ids.reshape(pair_total)
    onehot = (flat_ids[:, None] == jnp.arange(experts, dtype=jnp.int32)[None, :]).astype(jnp.int32)
    earlier = jnp.cumsum(onehot, axis=0) - onehot
    position = jnp.sum(earlier * onehot, axis=1)
    return (flat_ids * capacity + position).reshape(tok_count, top_count)


def per_device(tokens, expert_ids, combine, weight_gate, weight_up, weight_down, grad_out):
    tok_count, top_count = expert_ids.shape
    model_width = tokens.shape[1]
    experts = lax.axis_size("expert")
    copies = lax.axis_size("dp")
    capacity = 2 * tok_count * top_count // experts
    slots = experts * capacity
    target = slot_targets(expert_ids, experts, capacity)
    slot_iota = jnp.arange(slots, dtype=jnp.int32)
    hit = target.T[:, :, None] == slot_iota[None, None, :]
    send_onehot = jnp.any(hit, axis=0).T.astype(jnp.bfloat16)
    weight_pair = jnp.sum(
        jnp.where(hit, combine.T[:, :, None], jnp.zeros((), jnp.float32)), axis=(0, 1)
    )
    with jax.named_scope("dispatch_rows"):
        send_rows = jnp.dot(send_onehot, tokens, preferred_element_type=jnp.float32).astype(
            jnp.bfloat16
        )
        send_go = jnp.dot(send_onehot, grad_out, preferred_element_type=jnp.float32)
        send_grads = (weight_pair[:, None] * send_go).astype(jnp.bfloat16)
    send_rows = send_rows.reshape(experts, capacity, model_width)
    send_grads = send_grads.reshape(experts, capacity, model_width)
    recv_rows = lax.all_to_all(send_rows, "expert", split_axis=0, concat_axis=0, tiled=True)
    recv_rows, send_grads = lax.optimization_barrier((recv_rows, send_grads))
    recv_grads = lax.all_to_all(send_grads, "expert", split_axis=0, concat_axis=0, tiled=True)
    in_rows = recv_rows.reshape(slots, model_width)
    out_grads = recv_grads.reshape(slots, model_width)
    w_gate = weight_gate[0]
    w_up = weight_up[0]
    w_down = weight_down[0]
    def forward(rows):
        gate_pre = jnp.dot(rows, w_gate.T, preferred_element_type=jnp.float32)
        up_pre = jnp.dot(rows, w_up.T, preferred_element_type=jnp.float32)
        sigmoid_gate = jax.nn.sigmoid(gate_pre)
        activated = (gate_pre * sigmoid_gate * up_pre).astype(jnp.bfloat16)
        expert_out = jnp.dot(activated, w_down, preferred_element_type=jnp.float32).astype(
            jnp.bfloat16
        )
        return gate_pre, up_pre, sigmoid_gate, activated, expert_out

    always = expert_ids[0, 0] >= 0
    gate_pre, up_pre, sigmoid_gate, activated, expert_out = lax.cond(
        always, forward, forward, in_rows
    )
    me = lax.axis_index("expert")
    expert_out, out_grads = lax.optimization_barrier((expert_out, out_grads))
    back_out = []
    for shift in range(experts):
        chunk = lax.dynamic_slice_in_dim(expert_out, ((me + shift) % experts) * capacity, capacity, 0)
        if shift:
            chunk = lax.ppermute(
                chunk, "expert", [(j, (j + shift) % experts) for j in range(experts)]
            )
        back_out.append(chunk)
    back_out = jnp.concatenate(back_out, axis=0)
    scale = (tok_count * top_count * copies) ** (-0.5)
    grad_act = jnp.dot(out_grads, w_down.T, preferred_element_type=jnp.float32)
    grad_gate_pre = (
        grad_act * up_pre * sigmoid_gate * (1.0 + gate_pre * (1.0 - sigmoid_gate))
    ).astype(jnp.bfloat16)
    grad_up_pre = (grad_act * gate_pre * sigmoid_gate).astype(jnp.bfloat16)
    row_grads = (
        jnp.dot(grad_gate_pre, w_gate, preferred_element_type=jnp.float32)
        + jnp.dot(grad_up_pre, w_up, preferred_element_type=jnp.float32)
    ).astype(jnp.bfloat16)
    row_grads, back_out = lax.optimization_barrier((row_grads, back_out))
    back_grads = lax.all_to_all(
        row_grads.reshape(experts, capacity, model_width),
        "expert",
        split_axis=0,
        concat_axis=0,
        tiled=True,
    )
    ff_share = w_gate.shape[0] // copies
    with jax.named_scope("weight_grads"):
        down_term = (
            scale * jnp.einsum("rf,rd->fd", activated, out_grads, preferred_element_type=jnp.float32)
        ).astype(jnp.bfloat16)
        down_term, grad_gate_pre, grad_up_pre = lax.optimization_barrier(
            (down_term, grad_gate_pre, grad_up_pre)
        )
        gate_up_pre = jnp.stack(
            [
                grad_gate_pre.reshape(slots, copies, ff_share),
                grad_up_pre.reshape(slots, copies, ff_share),
            ],
            axis=2,
        ).reshape(slots, copies * 2 * ff_share)
        gate_up_term = (
            scale * jnp.einsum("rf,rd->fd", gate_up_pre, in_rows, preferred_element_type=jnp.float32)
        ).astype(jnp.bfloat16)
    down_share = lax.psum_scatter(down_term, "dp", scatter_dimension=0, tiled=True)
    gate_up_share = lax.psum_scatter(gate_up_term, "dp", scatter_dimension=0, tiled=True)
    gate_share = gate_up_share[:ff_share]
    up_share = gate_up_share[ff_share:]
    pick_onehot = hit.reshape(top_count * tok_count, slots).astype(jnp.bfloat16)
    with jax.named_scope("combine_rows"):
        shift_target = ((me - expert_ids) % experts) * capacity + target % capacity
        shift_onehot = (
            (shift_target.T[:, :, None] == slot_iota[None, None, :])
            .reshape(top_count * tok_count, slots)
            .astype(jnp.bfloat16)
        )
        picked_out = jnp.dot(shift_onehot, back_out, preferred_element_type=jnp.float32).reshape(
            top_count, tok_count, model_width
        )
        grad_f32 = grad_out.astype(jnp.float32)
        mixed = combine[:, 0:1] * picked_out[0]
        for k in range(1, top_count):
            mixed = mixed + combine[:, k : k + 1] * picked_out[k]
        mixed = mixed.astype(jnp.bfloat16)
        grad_combine = jnp.stack(
            [jnp.sum(grad_f32 * picked_out[k], axis=1) for k in range(top_count)], axis=1
        )
        back_grads, gate_share, up_share, mixed, grad_combine = lax.optimization_barrier(
            (back_grads, gate_share, up_share, mixed, grad_combine)
        )
        picked_grads = jnp.dot(
            pick_onehot, back_grads.reshape(slots, model_width), preferred_element_type=jnp.float32
        ).reshape(top_count, tok_count, model_width)
        grad_tokens = picked_grads[0]
        for k in range(1, top_count):
            grad_tokens = grad_tokens + picked_grads[k]
        grad_tokens = grad_tokens.astype(jnp.bfloat16)
    return (mixed, grad_tokens, grad_combine, gate_share[None], up_share[None], down_share[None])


def solution(mesh):
    in_specs = (
        P(("dp", "expert"), None),
        P(("dp", "expert"), None),
        P(("dp", "expert"), None),
        P("expert", None, None),
        P("expert", None, None),
        P("expert", None, None),
        P(("dp", "expert"), None),
    )
    out_specs = (
        P(("dp", "expert"), None),
        P(("dp", "expert"), None),
        P(("dp", "expert"), None),
        P("expert", "dp", None),
        P("expert", "dp", None),
        P("expert", "dp", None),
    )
    return jax.shard_map(
        per_device, mesh=mesh, in_specs=in_specs, out_specs=out_specs, check_vma=False
    )
```

```python
import jax
import jax.numpy as jnp
from jax import lax
from jax.sharding import PartitionSpec as P


def slot_targets(expert_ids, experts, capacity):
    tok_count, top_count = expert_ids.shape
    pair_total = tok_count * top_count
    flat_ids = expert_ids.reshape(pair_total)
    onehot = (flat_ids[:, None] == jnp.arange(experts, dtype=jnp.int32)[None, :]).astype(jnp.int32)
    earlier = jnp.cumsum(onehot, axis=0) - onehot
    position = jnp.sum(earlier * onehot, axis=1)
    return (flat_ids * capacity + position).reshape(tok_count, top_count)


def per_device(tokens, expert_ids, combine, weight_gate, weight_up, weight_down, grad_out):
    tok_count, top_count = expert_ids.shape
    model_width = tokens.shape[1]
    experts = lax.axis_size("expert")
    copies = lax.axis_size("dp")
    capacity = 2 * tok_count * top_count // experts
    slots = experts * capacity
    target = slot_targets(expert_ids, experts, capacity)
    slot_iota = jnp.arange(slots, dtype=jnp.int32)
    hit = target.T[:, :, None] == slot_iota[None, None, :]
    send_onehot = jnp.any(hit, axis=0).T.astype(jnp.bfloat16)
    weight_pair = jnp.sum(
        jnp.where(hit, combine.T[:, :, None], jnp.zeros((), jnp.float32)), axis=(0, 1)
    )
    with jax.named_scope("dispatch_rows"):
        send_rows = jnp.dot(send_onehot, tokens, preferred_element_type=jnp.float32).astype(
            jnp.bfloat16
        )
        send_go = jnp.dot(send_onehot, grad_out, preferred_element_type=jnp.float32)
        send_grads = (weight_pair[:, None] * send_go).astype(jnp.bfloat16)
    send_rows = send_rows.reshape(experts, capacity, model_width)
    send_grads = send_grads.reshape(experts, capacity, model_width)
    recv_rows = lax.all_to_all(send_rows, "expert", split_axis=0, concat_axis=0, tiled=True)
    recv_rows, send_grads = lax.optimization_barrier((recv_rows, send_grads))
    recv_grads = lax.all_to_all(send_grads, "expert", split_axis=0, concat_axis=0, tiled=True)
    in_rows = recv_rows.reshape(slots, model_width)
    out_grads = recv_grads.reshape(slots, model_width)
    w_gate = weight_gate[0]
    w_up = weight_up[0]
    w_down = weight_down[0]
    def forward(rows):
        gate_pre = jnp.dot(rows, w_gate.T, preferred_element_type=jnp.float32)
        up_pre = jnp.dot(rows, w_up.T, preferred_element_type=jnp.float32)
        sigmoid_gate = jax.nn.sigmoid(gate_pre)
        activated = (gate_pre * sigmoid_gate * up_pre).astype(jnp.bfloat16)
        expert_out = jnp.dot(activated, w_down, preferred_element_type=jnp.float32).astype(
            jnp.bfloat16
        )
        return gate_pre, up_pre, sigmoid_gate, activated, expert_out

    always = expert_ids[0, 0] >= 0
    gate_pre, up_pre, sigmoid_gate, activated, expert_out = lax.cond(
        always, forward, forward, in_rows
    )
    back_out = lax.all_to_all(
        expert_out.reshape(experts, capacity, model_width),
        "expert",
        split_axis=0,
        concat_axis=0,
        tiled=True,
    )
    scale = (tok_count * top_count * copies) ** (-0.5)
    grad_act = jnp.dot(out_grads, w_down.T, preferred_element_type=jnp.float32)
    grad_gate_pre = (
        grad_act * up_pre * sigmoid_gate * (1.0 + gate_pre * (1.0 - sigmoid_gate))
    ).astype(jnp.bfloat16)
    grad_up_pre = (grad_act * gate_pre * sigmoid_gate).astype(jnp.bfloat16)
    row_grads = (
        jnp.dot(grad_gate_pre, w_gate, preferred_element_type=jnp.float32)
        + jnp.dot(grad_up_pre, w_up, preferred_element_type=jnp.float32)
    ).astype(jnp.bfloat16)
    back_grads = lax.all_to_all(
        row_grads.reshape(experts, capacity, model_width),
        "expert",
        split_axis=0,
        concat_axis=0,
        tiled=True,
    )
    ff_share = w_gate.shape[0] // copies
    with jax.named_scope("weight_grads"):
        down_term = (
            scale * jnp.einsum("rf,rd->fd", activated, out_grads, preferred_element_type=jnp.float32)
        ).astype(jnp.bfloat16)
        rows_all = lax.all_gather(in_rows, "dp", axis=0, tiled=True)
        grads_pre = jnp.concatenate([grad_gate_pre, grad_up_pre], axis=1)
        grads_all = lax.all_gather(grads_pre, "dp", axis=0, tiled=True)
        me_dp = lax.axis_index("dp")
        ff = w_gate.shape[0]
        gate_cols = lax.dynamic_slice_in_dim(grads_all, me_dp * ff_share, ff_share, 1)
        up_cols = lax.dynamic_slice_in_dim(grads_all, ff + me_dp * ff_share, ff_share, 1)
        gate_share = (
            scale * jnp.einsum("rf,rd->fd", gate_cols, rows_all, preferred_element_type=jnp.float32)
        ).astype(jnp.bfloat16)
        up_share = (
            scale * jnp.einsum("rf,rd->fd", up_cols, rows_all, preferred_element_type=jnp.float32)
        ).astype(jnp.bfloat16)
    down_share = lax.psum_scatter(down_term, "dp", scatter_dimension=0, tiled=True)
    pick_onehot = hit.reshape(top_count * tok_count, slots).astype(jnp.bfloat16)
    with jax.named_scope("combine_rows"):
        picked_out = jnp.dot(
            pick_onehot, back_out.reshape(slots, model_width), preferred_element_type=jnp.float32
        ).reshape(top_count, tok_count, model_width)
        grad_f32 = grad_out.astype(jnp.float32)
        mixed = combine[:, 0:1] * picked_out[0]
        for k in range(1, top_count):
            mixed = mixed + combine[:, k : k + 1] * picked_out[k]
        mixed = mixed.astype(jnp.bfloat16)
        grad_combine = jnp.stack(
            [jnp.sum(grad_f32 * picked_out[k], axis=1) for k in range(top_count)], axis=1
        )
        back_grads, gate_share, up_share, mixed, grad_combine = lax.optimization_barrier(
            (back_grads, gate_share, up_share, mixed, grad_combine)
        )
        picked_grads = jnp.dot(
            pick_onehot, back_grads.reshape(slots, model_width), preferred_element_type=jnp.float32
        ).reshape(top_count, tok_count, model_width)
        grad_tokens = picked_grads[0]
        for k in range(1, top_count):
            grad_tokens = grad_tokens + picked_grads[k]
        grad_tokens = grad_tokens.astype(jnp.bfloat16)
    return (mixed, grad_tokens, grad_combine, gate_share[None], up_share[None], down_share[None])


def solution(mesh):
    in_specs = (
        P(("dp", "expert"), None),
        P(("dp", "expert"), None),
        P(("dp", "expert"), None),
        P("expert", None, None),
        P("expert", None, None),
        P("expert", None, None),
        P(("dp", "expert"), None),
    )
    out_specs = (
        P(("dp", "expert"), None),
        P(("dp", "expert"), None),
        P(("dp", "expert"), None),
        P("expert", "dp", None),
        P("expert", "dp", None),
        P("expert", "dp", None),
    )
    return jax.shard_map(
        per_device, mesh=mesh, in_specs=in_specs, out_specs=out_specs, check_vma=False
    )
```

```python
import jax
import jax.numpy as jnp
from jax import lax
from jax.sharding import PartitionSpec as P


def slot_targets(expert_ids, experts, capacity):
    tok_count, top_count = expert_ids.shape
    pair_total = tok_count * top_count
    flat_ids = expert_ids.reshape(pair_total)
    onehot = (flat_ids[:, None] == jnp.arange(experts, dtype=jnp.int32)[None, :]).astype(jnp.int32)
    earlier = jnp.cumsum(onehot, axis=0) - onehot
    position = jnp.sum(earlier * onehot, axis=1)
    return (flat_ids * capacity + position).reshape(tok_count, top_count)


def per_device(tokens, expert_ids, combine, weight_gate, weight_up, weight_down, grad_out):
    tok_count, top_count = expert_ids.shape
    model_width = tokens.shape[1]
    experts = lax.axis_size("expert")
    copies = lax.axis_size("dp")
    capacity = 2 * tok_count * top_count // experts
    slots = experts * capacity
    target = slot_targets(expert_ids, experts, capacity)
    slot_iota = jnp.arange(slots, dtype=jnp.int32)
    hit = target.T[:, :, None] == slot_iota[None, None, :]
    send_onehot = jnp.any(hit, axis=0).T.astype(jnp.bfloat16)
    weight_pair = jnp.sum(
        jnp.where(hit, combine.T[:, :, None], jnp.zeros((), jnp.float32)), axis=(0, 1)
    )
    with jax.named_scope("dispatch_rows"):
        send_rows = jnp.dot(send_onehot, tokens, preferred_element_type=jnp.float32).astype(
            jnp.bfloat16
        )
        send_go = jnp.dot(send_onehot, grad_out, preferred_element_type=jnp.float32)
        send_grads = (weight_pair[:, None] * send_go).astype(jnp.bfloat16)
    send_rows = send_rows.reshape(experts, capacity, model_width)
    send_grads = send_grads.reshape(experts, capacity, model_width)
    recv_rows = lax.all_to_all(send_rows, "expert", split_axis=0, concat_axis=0, tiled=True)
    recv_rows, send_grads = lax.optimization_barrier((recv_rows, send_grads))
    recv_grads = lax.all_to_all(send_grads, "expert", split_axis=0, concat_axis=0, tiled=True)
    in_rows = recv_rows.reshape(slots, model_width)
    out_grads = recv_grads.reshape(slots, model_width)
    w_gate = weight_gate[0]
    w_up = weight_up[0]
    w_down = weight_down[0]
    def forward(rows):
        gate_pre = jnp.dot(rows, w_gate.T, preferred_element_type=jnp.float32)
        up_pre = jnp.dot(rows, w_up.T, preferred_element_type=jnp.float32)
        sigmoid_gate = jax.nn.sigmoid(gate_pre)
        activated = (gate_pre * sigmoid_gate * up_pre).astype(jnp.bfloat16)
        expert_out = jnp.dot(activated, w_down, preferred_element_type=jnp.float32).astype(
            jnp.bfloat16
        )
        return gate_pre, up_pre, sigmoid_gate, activated, expert_out

    always = expert_ids[0, 0] >= 0
    gate_pre, up_pre, sigmoid_gate, activated, expert_out = lax.cond(
        always, forward, forward, in_rows
    )
    back_out = lax.all_to_all(
        expert_out.reshape(experts, capacity, model_width),
        "expert",
        split_axis=0,
        concat_axis=0,
        tiled=True,
    )
    scale = (tok_count * top_count * copies) ** (-0.5)
    grad_act = jnp.dot(out_grads, w_down.T, preferred_element_type=jnp.float32)
    grad_gate_pre = (
        grad_act * up_pre * sigmoid_gate * (1.0 + gate_pre * (1.0 - sigmoid_gate))
    ).astype(jnp.bfloat16)
    grad_up_pre = (grad_act * gate_pre * sigmoid_gate).astype(jnp.bfloat16)
    row_grads = (
        jnp.dot(grad_gate_pre, w_gate, preferred_element_type=jnp.float32)
        + jnp.dot(grad_up_pre, w_up, preferred_element_type=jnp.float32)
    ).astype(jnp.bfloat16)
    back_grads = lax.all_to_all(
        row_grads.reshape(experts, capacity, model_width),
        "expert",
        split_axis=0,
        concat_axis=0,
        tiled=True,
    )
    ff_share = w_gate.shape[0] // copies
    with jax.named_scope("weight_grads"):
        down_term = (
            scale * jnp.einsum("rf,rd->fd", activated, out_grads, preferred_element_type=jnp.float32)
        ).astype(jnp.bfloat16)
        gate_up_pre = jnp.stack(
            [
                grad_gate_pre.reshape(slots, copies, ff_share),
                grad_up_pre.reshape(slots, copies, ff_share),
            ],
            axis=2,
        ).reshape(slots, copies * 2 * ff_share)
        gate_up_term = (
            scale * jnp.einsum("rf,rd->fd", gate_up_pre, in_rows, preferred_element_type=jnp.float32)
        ).astype(jnp.bfloat16)
    down_share = lax.psum_scatter(down_term, "dp", scatter_dimension=0, tiled=True)
    gate_up_share = lax.psum_scatter(gate_up_term, "dp", scatter_dimension=0, tiled=True)
    gate_share = gate_up_share[:ff_share]
    up_share = gate_up_share[ff_share:]
    pick_onehot = hit.reshape(top_count * tok_count, slots).astype(jnp.bfloat16)
    with jax.named_scope("combine_rows"):
        picked_out = jnp.dot(
            pick_onehot, back_out.reshape(slots, model_width), preferred_element_type=jnp.float32
        ).reshape(top_count, tok_count, model_width)
        grad_f32 = grad_out.astype(jnp.float32)
        mixed = combine[:, 0:1] * picked_out[0]
        for k in range(1, top_count):
            mixed = mixed + combine[:, k : k + 1] * picked_out[k]
        mixed = mixed.astype(jnp.bfloat16)
        grad_combine = jnp.stack(
            [jnp.sum(grad_f32 * picked_out[k], axis=1) for k in range(top_count)], axis=1
        )
        back_grads, gate_share, up_share, mixed, grad_combine = lax.optimization_barrier(
            (back_grads, gate_share, up_share, mixed, grad_combine)
        )
        token_onehot = send_onehot.T
        grad_tokens = jnp.dot(
            token_onehot, back_grads.reshape(slots, model_width), preferred_element_type=jnp.float32
        ).astype(jnp.bfloat16)
    return (mixed, grad_tokens, grad_combine, gate_share[None], up_share[None], down_share[None])


def solution(mesh):
    in_specs = (
        P(("dp", "expert"), None),
        P(("dp", "expert"), None),
        P(("dp", "expert"), None),
        P("expert", None, None),
        P("expert", None, None),
        P("expert", None, None),
        P(("dp", "expert"), None),
    )
    out_specs = (
        P(("dp", "expert"), None),
        P(("dp", "expert"), None),
        P(("dp", "expert"), None),
        P("expert", "dp", None),
        P("expert", "dp", None),
        P("expert", "dp", None),
    )
    return jax.shard_map(
        per_device, mesh=mesh, in_specs=in_specs, out_specs=out_specs, check_vma=False
    )
```

```python
import jax
import jax.numpy as jnp
from jax import lax
from jax.sharding import PartitionSpec as P


def slot_targets(expert_ids, experts, capacity):
    tok_count, top_count = expert_ids.shape
    pair_total = tok_count * top_count
    flat_ids = expert_ids.reshape(pair_total)
    onehot = (flat_ids[:, None] == jnp.arange(experts, dtype=jnp.int32)[None, :]).astype(jnp.int32)
    earlier = jnp.cumsum(onehot, axis=0) - onehot
    position = jnp.sum(earlier * onehot, axis=1)
    return (flat_ids * capacity + position).reshape(tok_count, top_count)


def per_device(tokens, expert_ids, combine, weight_gate, weight_up, weight_down, grad_out):
    tok_count, top_count = expert_ids.shape
    model_width = tokens.shape[1]
    experts = lax.axis_size("expert")
    copies = lax.axis_size("dp")
    capacity = 2 * tok_count * top_count // experts
    slots = experts * capacity
    target = slot_targets(expert_ids, experts, capacity)
    slot_iota = jnp.arange(slots, dtype=jnp.int32)
    hit = target.T[:, :, None] == slot_iota[None, None, :]
    send_onehot = jnp.any(hit, axis=0).T.astype(jnp.bfloat16)
    weight_pair = jnp.sum(
        jnp.where(hit, combine.T[:, :, None], jnp.zeros((), jnp.float32)), axis=(0, 1)
    )
    with jax.named_scope("dispatch_rows"):
        send_rows = jnp.dot(send_onehot, tokens, preferred_element_type=jnp.float32).astype(
            jnp.bfloat16
        )
        send_go = jnp.dot(send_onehot, grad_out, preferred_element_type=jnp.float32)
        send_grads = (weight_pair[:, None] * send_go).astype(jnp.bfloat16)
    send_rows = send_rows.reshape(experts, capacity, model_width)
    send_grads = send_grads.reshape(experts, capacity, model_width)
    recv_rows = lax.all_to_all(send_rows, "expert", split_axis=0, concat_axis=0, tiled=True)
    recv_rows, send_grads = lax.optimization_barrier((recv_rows, send_grads))
    recv_grads = lax.all_to_all(send_grads, "expert", split_axis=0, concat_axis=0, tiled=True)
    in_rows = recv_rows.reshape(slots, model_width)
    out_grads = recv_grads.reshape(slots, model_width)
    w_gate = weight_gate[0]
    w_up = weight_up[0]
    w_down = weight_down[0]
    def forward(rows):
        gate_pre = jnp.dot(rows, w_gate.T, preferred_element_type=jnp.float32)
        up_pre = jnp.dot(rows, w_up.T, preferred_element_type=jnp.float32)
        sigmoid_gate = jax.nn.sigmoid(gate_pre)
        activated = (gate_pre * sigmoid_gate * up_pre).astype(jnp.bfloat16)
        expert_out = jnp.dot(activated, w_down, preferred_element_type=jnp.float32).astype(
            jnp.bfloat16
        )
        return gate_pre, up_pre, sigmoid_gate, activated, expert_out

    always = expert_ids[0, 0] >= 0
    gate_pre, up_pre, sigmoid_gate, activated, expert_out = lax.cond(
        always, forward, forward, in_rows
    )
    back_out = lax.all_to_all(
        expert_out.reshape(experts, capacity, model_width),
        "expert",
        split_axis=0,
        concat_axis=0,
        tiled=True,
    )
    scale = (tok_count * top_count * copies) ** (-0.5)
    grad_act = jnp.dot(out_grads, w_down.T, preferred_element_type=jnp.float32)
    grad_gate_pre = (
        grad_act * up_pre * sigmoid_gate * (1.0 + gate_pre * (1.0 - sigmoid_gate))
    ).astype(jnp.bfloat16)
    grad_up_pre = (grad_act * gate_pre * sigmoid_gate).astype(jnp.bfloat16)
    row_grads = (
        jnp.dot(grad_gate_pre, w_gate, preferred_element_type=jnp.float32)
        + jnp.dot(grad_up_pre, w_up, preferred_element_type=jnp.float32)
    ).astype(jnp.bfloat16)
    me = lax.axis_index("expert")
    back_grads = []
    for shift in range(experts):
        chunk = lax.dynamic_slice_in_dim(row_grads, ((me + shift) % experts) * capacity, capacity, 0)
        if shift:
            chunk = lax.ppermute(
                chunk, "expert", [(j, (j + shift) % experts) for j in range(experts)]
            )
        back_grads.append(chunk)
    back_grads = jnp.concatenate(back_grads, axis=0)
    ff_share = w_gate.shape[0] // copies
    with jax.named_scope("weight_grads"):
        down_term = (
            scale * jnp.einsum("rf,rd->fd", activated, out_grads, preferred_element_type=jnp.float32)
        ).astype(jnp.bfloat16)
        gate_up_pre = jnp.stack(
            [
                grad_gate_pre.reshape(slots, copies, ff_share),
                grad_up_pre.reshape(slots, copies, ff_share),
            ],
            axis=2,
        ).reshape(slots, copies * 2 * ff_share)
        gate_up_term = (
            scale * jnp.einsum("rf,rd->fd", gate_up_pre, in_rows, preferred_element_type=jnp.float32)
        ).astype(jnp.bfloat16)
    down_share = lax.psum_scatter(down_term, "dp", scatter_dimension=0, tiled=True)
    gate_up_share = lax.psum_scatter(gate_up_term, "dp", scatter_dimension=0, tiled=True)
    gate_share = gate_up_share[:ff_share]
    up_share = gate_up_share[ff_share:]
    pick_onehot = hit.reshape(top_count * tok_count, slots).astype(jnp.bfloat16)
    with jax.named_scope("combine_rows"):
        picked_out = jnp.dot(
            pick_onehot, back_out.reshape(slots, model_width), preferred_element_type=jnp.float32
        ).reshape(top_count, tok_count, model_width)
        grad_f32 = grad_out.astype(jnp.float32)
        mixed = combine[:, 0:1] * picked_out[0]
        for k in range(1, top_count):
            mixed = mixed + combine[:, k : k + 1] * picked_out[k]
        mixed = mixed.astype(jnp.bfloat16)
        grad_combine = jnp.stack(
            [jnp.sum(grad_f32 * picked_out[k], axis=1) for k in range(top_count)], axis=1
        )
        back_grads, gate_share, up_share, mixed, grad_combine = lax.optimization_barrier(
            (back_grads, gate_share, up_share, mixed, grad_combine)
        )
        shift_target = ((me - expert_ids) % experts) * capacity + target % capacity
        token_onehot = jnp.any(
            shift_target[:, :, None] == slot_iota[None, None, :], axis=1
        ).astype(jnp.bfloat16)
        grad_tokens = jnp.dot(
            token_onehot, back_grads.reshape(slots, model_width), preferred_element_type=jnp.float32
        ).astype(jnp.bfloat16)
    return (mixed, grad_tokens, grad_combine, gate_share[None], up_share[None], down_share[None])


def solution(mesh):
    in_specs = (
        P(("dp", "expert"), None),
        P(("dp", "expert"), None),
        P(("dp", "expert"), None),
        P("expert", None, None),
        P("expert", None, None),
        P("expert", None, None),
        P(("dp", "expert"), None),
    )
    out_specs = (
        P(("dp", "expert"), None),
        P(("dp", "expert"), None),
        P(("dp", "expert"), None),
        P("expert", "dp", None),
        P("expert", "dp", None),
        P("expert", "dp", None),
    )
    return jax.shard_map(
        per_device, mesh=mesh, in_specs=in_specs, out_specs=out_specs, check_vma=False
    )
```

```python
import jax
import jax.numpy as jnp
from jax import lax
from jax.sharding import PartitionSpec as P


def slot_targets(expert_ids, experts, capacity):
    tok_count, top_count = expert_ids.shape
    pair_total = tok_count * top_count
    flat_ids = expert_ids.reshape(pair_total)
    onehot = (flat_ids[:, None] == jnp.arange(experts, dtype=jnp.int32)[None, :]).astype(jnp.int32)
    earlier = jnp.cumsum(onehot, axis=0) - onehot
    position = jnp.sum(earlier * onehot, axis=1)
    return (flat_ids * capacity + position).reshape(tok_count, top_count)


def per_device(tokens, expert_ids, combine, weight_gate, weight_up, weight_down, grad_out):
    tok_count, top_count = expert_ids.shape
    model_width = tokens.shape[1]
    experts = lax.axis_size("expert")
    copies = lax.axis_size("dp")
    capacity = 2 * tok_count * top_count // experts
    slots = experts * capacity
    target = slot_targets(expert_ids, experts, capacity)
    slot_iota = jnp.arange(slots, dtype=jnp.int32)
    hit = target.T[:, :, None] == slot_iota[None, None, :]
    send_onehot = jnp.any(hit, axis=0).T.astype(jnp.bfloat16)
    weight_pair = jnp.sum(
        jnp.where(hit, combine.T[:, :, None], jnp.zeros((), jnp.float32)), axis=(0, 1)
    )
    with jax.named_scope("dispatch_rows"):
        send_rows = jnp.dot(send_onehot, tokens, preferred_element_type=jnp.float32).astype(
            jnp.bfloat16
        )
        send_go = jnp.dot(send_onehot, grad_out, preferred_element_type=jnp.float32)
        send_grads = (weight_pair[:, None] * send_go).astype(jnp.bfloat16)
    send_rows = send_rows.reshape(experts, capacity, model_width)
    send_grads = send_grads.reshape(experts, capacity, model_width)
    recv_rows = lax.all_to_all(send_rows, "expert", split_axis=0, concat_axis=0, tiled=True)
    recv_rows, send_grads = lax.optimization_barrier((recv_rows, send_grads))
    recv_grads = lax.all_to_all(send_grads, "expert", split_axis=0, concat_axis=0, tiled=True)
    in_rows = recv_rows.reshape(slots, model_width)
    out_grads = recv_grads.reshape(slots, model_width)
    w_gate = weight_gate[0]
    w_up = weight_up[0]
    w_down = weight_down[0]
    def forward(rows):
        gate_pre = jnp.dot(rows, w_gate.T, preferred_element_type=jnp.float32)
        up_pre = jnp.dot(rows, w_up.T, preferred_element_type=jnp.float32)
        sigmoid_gate = jax.nn.sigmoid(gate_pre)
        activated = (gate_pre * sigmoid_gate * up_pre).astype(jnp.bfloat16)
        expert_out = jnp.dot(activated, w_down, preferred_element_type=jnp.float32).astype(
            jnp.bfloat16
        )
        return gate_pre, up_pre, sigmoid_gate, activated, expert_out

    always = expert_ids[0, 0] >= 0
    gate_pre, up_pre, sigmoid_gate, activated, expert_out = lax.cond(
        always, forward, forward, in_rows
    )
    back_out = lax.all_to_all(
        expert_out.reshape(experts, capacity, model_width),
        "expert",
        split_axis=0,
        concat_axis=0,
        tiled=True,
    )
    scale = (tok_count * top_count * copies) ** (-0.5)
    grad_act = jnp.dot(out_grads, w_down.T, preferred_element_type=jnp.float32)
    grad_gate_pre = (
        grad_act * up_pre * sigmoid_gate * (1.0 + gate_pre * (1.0 - sigmoid_gate))
    ).astype(jnp.bfloat16)
    grad_up_pre = (grad_act * gate_pre * sigmoid_gate).astype(jnp.bfloat16)
    row_grads = (
        jnp.dot(grad_gate_pre, w_gate, preferred_element_type=jnp.float32)
        + jnp.dot(grad_up_pre, w_up, preferred_element_type=jnp.float32)
    ).astype(jnp.bfloat16)
    ff_share = w_gate.shape[0] // copies
    with jax.named_scope("weight_grads"):
        down_term = (
            scale * jnp.einsum("rf,rd->fd", activated, out_grads, preferred_element_type=jnp.float32)
        ).astype(jnp.bfloat16)
        gate_up_pre = jnp.stack(
            [
                grad_gate_pre.reshape(slots, copies, ff_share),
                grad_up_pre.reshape(slots, copies, ff_share),
            ],
            axis=2,
        ).reshape(slots, copies * 2 * ff_share)
        gate_up_term = (
            scale * jnp.einsum("rf,rd->fd", gate_up_pre, in_rows, preferred_element_type=jnp.float32)
        ).astype(jnp.bfloat16)
    down_share = lax.psum_scatter(down_term, "dp", scatter_dimension=0, tiled=True)
    gate_up_share = lax.psum_scatter(gate_up_term, "dp", scatter_dimension=0, tiled=True)
    gate_share = gate_up_share[:ff_share]
    up_share = gate_up_share[ff_share:]
    me = lax.axis_index("expert")
    back_grads = []
    for shift in range(experts):
        chunk = lax.dynamic_slice_in_dim(row_grads, ((me + shift) % experts) * capacity, capacity, 0)
        if shift == experts // 2:
            chunk, gate_share, up_share = lax.optimization_barrier((chunk, gate_share, up_share))
        if shift:
            chunk = lax.ppermute(
                chunk, "expert", [(j, (j + shift) % experts) for j in range(experts)]
            )
        back_grads.append(chunk)
    back_grads = jnp.concatenate(back_grads, axis=0)
    pick_onehot = hit.reshape(top_count * tok_count, slots).astype(jnp.bfloat16)
    with jax.named_scope("combine_rows"):
        picked_out = jnp.dot(
            pick_onehot, back_out.reshape(slots, model_width), preferred_element_type=jnp.float32
        ).reshape(top_count, tok_count, model_width)
        grad_f32 = grad_out.astype(jnp.float32)
        mixed = combine[:, 0:1] * picked_out[0]
        for k in range(1, top_count):
            mixed = mixed + combine[:, k : k + 1] * picked_out[k]
        mixed = mixed.astype(jnp.bfloat16)
        grad_combine = jnp.stack(
            [jnp.sum(grad_f32 * picked_out[k], axis=1) for k in range(top_count)], axis=1
        )
        back_grads, gate_share, up_share, mixed, grad_combine = lax.optimization_barrier(
            (back_grads, gate_share, up_share, mixed, grad_combine)
        )
        shift_target = ((me - expert_ids) % experts) * capacity + target % capacity
        token_onehot = jnp.any(
            shift_target[:, :, None] == slot_iota[None, None, :], axis=1
        ).astype(jnp.bfloat16)
        grad_tokens = jnp.dot(
            token_onehot, back_grads.reshape(slots, model_width), preferred_element_type=jnp.float32
        ).astype(jnp.bfloat16)
    return (mixed, grad_tokens, grad_combine, gate_share[None], up_share[None], down_share[None])


def solution(mesh):
    in_specs = (
        P(("dp", "expert"), None),
        P(("dp", "expert"), None),
        P(("dp", "expert"), None),
        P("expert", None, None),
        P("expert", None, None),
        P("expert", None, None),
        P(("dp", "expert"), None),
    )
    out_specs = (
        P(("dp", "expert"), None),
        P(("dp", "expert"), None),
        P(("dp", "expert"), None),
        P("expert", "dp", None),
        P("expert", "dp", None),
        P("expert", "dp", None),
    )
    return jax.shard_map(
        per_device, mesh=mesh, in_specs=in_specs, out_specs=out_specs, check_vma=False
    )
```

```python
import jax
import jax.numpy as jnp
from jax import lax
from jax.sharding import PartitionSpec as P


def slot_targets(expert_ids, experts, capacity):
    tok_count, top_count = expert_ids.shape
    pair_total = tok_count * top_count
    flat_ids = expert_ids.reshape(pair_total)
    onehot = (flat_ids[:, None] == jnp.arange(experts, dtype=jnp.int32)[None, :]).astype(jnp.int32)
    earlier = jnp.cumsum(onehot, axis=0) - onehot
    position = jnp.sum(earlier * onehot, axis=1)
    return (flat_ids * capacity + position).reshape(tok_count, top_count)


def per_device(tokens, expert_ids, combine, weight_gate, weight_up, weight_down, grad_out):
    tok_count, top_count = expert_ids.shape
    model_width = tokens.shape[1]
    experts = lax.axis_size("expert")
    copies = lax.axis_size("dp")
    capacity = 2 * tok_count * top_count // experts
    slots = experts * capacity
    target = slot_targets(expert_ids, experts, capacity)
    slot_iota = jnp.arange(slots, dtype=jnp.int32)
    hit = target.T[:, :, None] == slot_iota[None, None, :]
    send_onehot = jnp.any(hit, axis=0).T.astype(jnp.bfloat16)
    weight_pair = jnp.sum(
        jnp.where(hit, combine.T[:, :, None], jnp.zeros((), jnp.float32)), axis=(0, 1)
    )
    with jax.named_scope("dispatch_rows"):
        send_rows = jnp.dot(send_onehot, tokens, preferred_element_type=jnp.float32).astype(
            jnp.bfloat16
        )
        send_go = jnp.dot(send_onehot, grad_out, preferred_element_type=jnp.float32)
        send_grads = (weight_pair[:, None] * send_go).astype(jnp.bfloat16)
    send_rows = send_rows.reshape(experts, capacity, model_width)
    send_grads = send_grads.reshape(experts, capacity, model_width)
    recv_rows = lax.all_to_all(send_rows, "expert", split_axis=0, concat_axis=0, tiled=True)
    recv_rows, send_grads = lax.optimization_barrier((recv_rows, send_grads))
    recv_grads = lax.all_to_all(send_grads, "expert", split_axis=0, concat_axis=0, tiled=True)
    in_rows = recv_rows.reshape(slots, model_width)
    out_grads = recv_grads.reshape(slots, model_width)
    w_gate = weight_gate[0]
    w_up = weight_up[0]
    w_down = weight_down[0]
    def forward(rows):
        gate_pre = jnp.dot(rows, w_gate.T, preferred_element_type=jnp.float32)
        up_pre = jnp.dot(rows, w_up.T, preferred_element_type=jnp.float32)
        sigmoid_gate = jax.nn.sigmoid(gate_pre)
        activated = (gate_pre * sigmoid_gate * up_pre).astype(jnp.bfloat16)
        expert_out = jnp.dot(activated, w_down, preferred_element_type=jnp.float32).astype(
            jnp.bfloat16
        )
        return gate_pre, up_pre, sigmoid_gate, activated, expert_out

    always = expert_ids[0, 0] >= 0
    gate_pre, up_pre, sigmoid_gate, activated, expert_out = lax.cond(
        always, forward, forward, in_rows
    )
    back_out = lax.all_to_all(
        expert_out.reshape(experts, capacity, model_width),
        "expert",
        split_axis=0,
        concat_axis=0,
        tiled=True,
    )
    scale = (tok_count * top_count * copies) ** (-0.5)
    grad_act = jnp.dot(out_grads, w_down.T, preferred_element_type=jnp.float32)
    grad_gate_pre = (
        grad_act * up_pre * sigmoid_gate * (1.0 + gate_pre * (1.0 - sigmoid_gate))
    ).astype(jnp.bfloat16)
    grad_up_pre = (grad_act * gate_pre * sigmoid_gate).astype(jnp.bfloat16)
    row_grads = (
        jnp.dot(grad_gate_pre, w_gate, preferred_element_type=jnp.float32)
        + jnp.dot(grad_up_pre, w_up, preferred_element_type=jnp.float32)
    ).astype(jnp.bfloat16)
    ff_share = w_gate.shape[0] // copies
    with jax.named_scope("weight_grads"):
        down_term = (
            scale * jnp.einsum("rf,rd->fd", activated, out_grads, preferred_element_type=jnp.float32)
        ).astype(jnp.bfloat16)
        gate_up_pre = jnp.stack(
            [
                grad_gate_pre.reshape(slots, copies, ff_share),
                grad_up_pre.reshape(slots, copies, ff_share),
            ],
            axis=2,
        ).reshape(slots, copies * 2 * ff_share)
        gate_up_term = (
            scale * jnp.einsum("rf,rd->fd", gate_up_pre, in_rows, preferred_element_type=jnp.float32)
        ).astype(jnp.bfloat16)
    down_share = lax.psum_scatter(down_term, "dp", scatter_dimension=0, tiled=True)
    gate_up_share = lax.psum_scatter(gate_up_term, "dp", scatter_dimension=0, tiled=True)
    gate_share = gate_up_share[:ff_share]
    up_share = gate_up_share[ff_share:]
    me = lax.axis_index("expert")
    back_grads = []
    for shift in range(experts):
        chunk = lax.dynamic_slice_in_dim(row_grads, ((me + shift) % experts) * capacity, capacity, 0)
        if shift == experts // 2:
            chunk, gate_share, up_share = lax.optimization_barrier((chunk, gate_share, up_share))
        if shift:
            chunk = lax.ppermute(
                chunk, "expert", [(j, (j + shift) % experts) for j in range(experts)]
            )
        back_grads.append(chunk)
    back_grads = jnp.concatenate(back_grads, axis=0)
    pick_onehot = hit.reshape(top_count * tok_count, slots).astype(jnp.bfloat16)
    with jax.named_scope("combine_rows"):
        picked_out = jnp.dot(
            pick_onehot, back_out.reshape(slots, model_width), preferred_element_type=jnp.float32
        ).reshape(top_count, tok_count, model_width)
        grad_f32 = grad_out.astype(jnp.float32)
        mixed = combine[:, 0:1] * picked_out[0]
        for k in range(1, top_count):
            mixed = mixed + combine[:, k : k + 1] * picked_out[k]
        mixed = mixed.astype(jnp.bfloat16)
        grad_combine = jnp.stack(
            [jnp.sum(grad_f32 * picked_out[k], axis=1) for k in range(top_count)], axis=1
        )
        back_grads, gate_share, up_share, mixed, grad_combine = lax.optimization_barrier(
            (back_grads, gate_share, up_share, mixed, grad_combine)
        )
        shift_target = ((me - expert_ids) % experts) * capacity + target % capacity
        grad_tokens = back_grads[shift_target[:, 0]].astype(jnp.float32)
        for k in range(1, top_count):
            grad_tokens = grad_tokens + back_grads[shift_target[:, k]].astype(jnp.float32)
        grad_tokens = grad_tokens.astype(jnp.bfloat16)
    return (mixed, grad_tokens, grad_combine, gate_share[None], up_share[None], down_share[None])


def solution(mesh):
    in_specs = (
        P(("dp", "expert"), None),
        P(("dp", "expert"), None),
        P(("dp", "expert"), None),
        P("expert", None, None),
        P("expert", None, None),
        P("expert", None, None),
        P(("dp", "expert"), None),
    )
    out_specs = (
        P(("dp", "expert"), None),
        P(("dp", "expert"), None),
        P(("dp", "expert"), None),
        P("expert", "dp", None),
        P("expert", "dp", None),
        P("expert", "dp", None),
    )
    return jax.shard_map(
        per_device, mesh=mesh, in_specs=in_specs, out_specs=out_specs, check_vma=False
    )
```

```python
import jax
import jax.numpy as jnp
from jax import lax
from jax.sharding import PartitionSpec as P


def slot_targets(expert_ids, experts, capacity):
    tok_count, top_count = expert_ids.shape
    pair_total = tok_count * top_count
    flat_ids = expert_ids.reshape(pair_total)
    onehot = flat_ids[:, None] == jnp.arange(experts, dtype=jnp.int32)[None, :]
    pair_iota = jnp.arange(pair_total, dtype=jnp.int32)
    before = (pair_iota[None, :] < pair_iota[:, None]).astype(jnp.bfloat16)
    earlier = jnp.dot(before, onehot.astype(jnp.bfloat16), preferred_element_type=jnp.float32)
    position = jnp.sum(jnp.where(onehot, earlier, 0.0), axis=1).astype(jnp.int32)
    return (flat_ids * capacity + position).reshape(tok_count, top_count)


def per_device(tokens, expert_ids, combine, weight_gate, weight_up, weight_down, grad_out):
    tok_count, top_count = expert_ids.shape
    model_width = tokens.shape[1]
    experts = lax.axis_size("expert")
    copies = lax.axis_size("dp")
    capacity = 2 * tok_count * top_count // experts
    slots = experts * capacity
    target = slot_targets(expert_ids, experts, capacity)
    slot_iota = jnp.arange(slots, dtype=jnp.int32)
    hit = target.T[:, :, None] == slot_iota[None, None, :]
    send_onehot = jnp.any(hit, axis=0).T.astype(jnp.bfloat16)
    weight_pair = jnp.sum(
        jnp.where(hit, combine.T[:, :, None], jnp.zeros((), jnp.float32)), axis=(0, 1)
    )
    with jax.named_scope("dispatch_rows"):
        send_rows = jnp.dot(send_onehot, tokens, preferred_element_type=jnp.float32).astype(
            jnp.bfloat16
        )
        send_go = jnp.dot(send_onehot, grad_out, preferred_element_type=jnp.float32)
        send_grads = (weight_pair[:, None] * send_go).astype(jnp.bfloat16)
    send_rows = send_rows.reshape(experts, capacity, model_width)
    send_grads = send_grads.reshape(experts, capacity, model_width)
    recv_rows = lax.all_to_all(send_rows, "expert", split_axis=0, concat_axis=0, tiled=True)
    recv_rows, send_grads = lax.optimization_barrier((recv_rows, send_grads))
    recv_grads = lax.all_to_all(send_grads, "expert", split_axis=0, concat_axis=0, tiled=True)
    in_rows = recv_rows.reshape(slots, model_width)
    out_grads = recv_grads.reshape(slots, model_width)
    w_gate = weight_gate[0]
    w_up = weight_up[0]
    w_down = weight_down[0]
    def forward(rows):
        gate_pre = jnp.dot(rows, w_gate.T, preferred_element_type=jnp.float32)
        up_pre = jnp.dot(rows, w_up.T, preferred_element_type=jnp.float32)
        sigmoid_gate = jax.nn.sigmoid(gate_pre)
        activated = (gate_pre * sigmoid_gate * up_pre).astype(jnp.bfloat16)
        expert_out = jnp.dot(activated, w_down, preferred_element_type=jnp.float32).astype(
            jnp.bfloat16
        )
        return gate_pre, up_pre, sigmoid_gate, activated, expert_out

    always = expert_ids[0, 0] >= 0
    gate_pre, up_pre, sigmoid_gate, activated, expert_out = lax.cond(
        always, forward, forward, in_rows
    )
    back_out = lax.all_to_all(
        expert_out.reshape(experts, capacity, model_width),
        "expert",
        split_axis=0,
        concat_axis=0,
        tiled=True,
    )
    scale = (tok_count * top_count * copies) ** (-0.5)
    grad_act = jnp.dot(out_grads, w_down.T, preferred_element_type=jnp.float32)
    grad_gate_pre = (
        grad_act * up_pre * sigmoid_gate * (1.0 + gate_pre * (1.0 - sigmoid_gate))
    ).astype(jnp.bfloat16)
    grad_up_pre = (grad_act * gate_pre * sigmoid_gate).astype(jnp.bfloat16)
    row_grads = (
        jnp.dot(grad_gate_pre, w_gate, preferred_element_type=jnp.float32)
        + jnp.dot(grad_up_pre, w_up, preferred_element_type=jnp.float32)
    ).astype(jnp.bfloat16)
    ff_share = w_gate.shape[0] // copies
    with jax.named_scope("weight_grads"):
        down_term = (
            scale * jnp.einsum("rf,rd->fd", activated, out_grads, preferred_element_type=jnp.float32)
        ).astype(jnp.bfloat16)
        gate_up_pre = jnp.stack(
            [
                grad_gate_pre.reshape(slots, copies, ff_share),
                grad_up_pre.reshape(slots, copies, ff_share),
            ],
            axis=2,
        ).reshape(slots, copies * 2 * ff_share)
        gate_up_term = (
            scale * jnp.einsum("rf,rd->fd", gate_up_pre, in_rows, preferred_element_type=jnp.float32)
        ).astype(jnp.bfloat16)
    down_share = lax.psum_scatter(down_term, "dp", scatter_dimension=0, tiled=True)
    gate_up_share = lax.psum_scatter(gate_up_term, "dp", scatter_dimension=0, tiled=True)
    gate_share = gate_up_share[:ff_share]
    up_share = gate_up_share[ff_share:]
    me = lax.axis_index("expert")
    back_grads = []
    for shift in range(experts):
        chunk = lax.dynamic_slice_in_dim(row_grads, ((me + shift) % experts) * capacity, capacity, 0)
        if shift == experts // 2:
            chunk, gate_share, up_share = lax.optimization_barrier((chunk, gate_share, up_share))
        if shift:
            chunk = lax.ppermute(
                chunk, "expert", [(j, (j + shift) % experts) for j in range(experts)]
            )
        back_grads.append(chunk)
    back_grads = jnp.concatenate(back_grads, axis=0)
    pick_onehot = hit.reshape(top_count * tok_count, slots).astype(jnp.bfloat16)
    with jax.named_scope("combine_rows"):
        picked_out = jnp.dot(
            pick_onehot, back_out.reshape(slots, model_width), preferred_element_type=jnp.float32
        ).reshape(top_count, tok_count, model_width)
        grad_f32 = grad_out.astype(jnp.float32)
        mixed = combine[:, 0:1] * picked_out[0]
        for k in range(1, top_count):
            mixed = mixed + combine[:, k : k + 1] * picked_out[k]
        mixed = mixed.astype(jnp.bfloat16)
        grad_combine = jnp.stack(
            [jnp.sum(grad_f32 * picked_out[k], axis=1) for k in range(top_count)], axis=1
        )
        back_grads, gate_share, up_share, mixed, grad_combine = lax.optimization_barrier(
            (back_grads, gate_share, up_share, mixed, grad_combine)
        )
        shift_target = ((me - expert_ids) % experts) * capacity + target % capacity
        token_onehot = jnp.any(
            shift_target[:, :, None] == slot_iota[None, None, :], axis=1
        ).astype(jnp.bfloat16)
        grad_tokens = jnp.dot(
            token_onehot, back_grads.reshape(slots, model_width), preferred_element_type=jnp.float32
        ).astype(jnp.bfloat16)
    return (mixed, grad_tokens, grad_combine, gate_share[None], up_share[None], down_share[None])


def solution(mesh):
    in_specs = (
        P(("dp", "expert"), None),
        P(("dp", "expert"), None),
        P(("dp", "expert"), None),
        P("expert", None, None),
        P("expert", None, None),
        P("expert", None, None),
        P(("dp", "expert"), None),
    )
    out_specs = (
        P(("dp", "expert"), None),
        P(("dp", "expert"), None),
        P(("dp", "expert"), None),
        P("expert", "dp", None),
        P("expert", "dp", None),
        P("expert", "dp", None),
    )
    return jax.shard_map(
        per_device, mesh=mesh, in_specs=in_specs, out_specs=out_specs, check_vma=False
    )
```

```python
import jax
import jax.numpy as jnp
from jax import lax
from jax.sharding import PartitionSpec as P


def slot_targets(expert_ids, experts, capacity):
    tok_count, top_count = expert_ids.shape
    pair_total = tok_count * top_count
    flat_ids = expert_ids.reshape(pair_total)
    onehot = flat_ids[:, None] == jnp.arange(experts, dtype=jnp.int32)[None, :]
    pair_iota = jnp.arange(pair_total, dtype=jnp.int32)
    before = (pair_iota[None, :] < pair_iota[:, None]).astype(jnp.bfloat16)
    earlier = jnp.dot(before, onehot.astype(jnp.bfloat16), preferred_element_type=jnp.float32)
    position = jnp.sum(jnp.where(onehot, earlier, 0.0), axis=1).astype(jnp.int32)
    return (flat_ids * capacity + position).reshape(tok_count, top_count)


def per_device(tokens, expert_ids, combine, weight_gate, weight_up, weight_down, grad_out):
    tok_count, top_count = expert_ids.shape
    model_width = tokens.shape[1]
    experts = lax.axis_size("expert")
    copies = lax.axis_size("dp")
    capacity = 2 * tok_count * top_count // experts
    slots = experts * capacity
    target = slot_targets(expert_ids, experts, capacity)
    slot_iota = jnp.arange(slots, dtype=jnp.int32)
    hit = target.T[:, :, None] == slot_iota[None, None, :]
    send_onehot = jnp.any(
        slot_iota[:, None, None] == target[None, :, :], axis=2
    ).astype(jnp.bfloat16)
    weight_pair = jnp.sum(
        jnp.where(hit, combine.T[:, :, None], jnp.zeros((), jnp.float32)), axis=(0, 1)
    )
    with jax.named_scope("dispatch_rows"):
        send_rows = jnp.dot(send_onehot, tokens, preferred_element_type=jnp.float32).astype(
            jnp.bfloat16
        )
        send_go = jnp.dot(send_onehot, grad_out, preferred_element_type=jnp.float32)
        send_grads = (weight_pair[:, None] * send_go).astype(jnp.bfloat16)
    send_rows = send_rows.reshape(experts, capacity, model_width)
    send_grads = send_grads.reshape(experts, capacity, model_width)
    recv_rows = lax.all_to_all(send_rows, "expert", split_axis=0, concat_axis=0, tiled=True)
    recv_rows, send_grads = lax.optimization_barrier((recv_rows, send_grads))
    recv_grads = lax.all_to_all(send_grads, "expert", split_axis=0, concat_axis=0, tiled=True)
    in_rows = recv_rows.reshape(slots, model_width)
    out_grads = recv_grads.reshape(slots, model_width)
    w_gate = weight_gate[0]
    w_up = weight_up[0]
    w_down = weight_down[0]
    def forward(rows):
        gate_pre = jnp.dot(rows, w_gate.T, preferred_element_type=jnp.float32)
        up_pre = jnp.dot(rows, w_up.T, preferred_element_type=jnp.float32)
        sigmoid_gate = jax.nn.sigmoid(gate_pre)
        activated = (gate_pre * sigmoid_gate * up_pre).astype(jnp.bfloat16)
        expert_out = jnp.dot(activated, w_down, preferred_element_type=jnp.float32).astype(
            jnp.bfloat16
        )
        return gate_pre, up_pre, sigmoid_gate, activated, expert_out

    always = expert_ids[0, 0] >= 0
    gate_pre, up_pre, sigmoid_gate, activated, expert_out = lax.cond(
        always, forward, forward, in_rows
    )
    back_out = lax.all_to_all(
        expert_out.reshape(experts, capacity, model_width),
        "expert",
        split_axis=0,
        concat_axis=0,
        tiled=True,
    )
    scale = (tok_count * top_count * copies) ** (-0.5)
    grad_act = jnp.dot(out_grads, w_down.T, preferred_element_type=jnp.float32)
    grad_gate_pre = (
        grad_act * up_pre * sigmoid_gate * (1.0 + gate_pre * (1.0 - sigmoid_gate))
    ).astype(jnp.bfloat16)
    grad_up_pre = (grad_act * gate_pre * sigmoid_gate).astype(jnp.bfloat16)
    row_grads = (
        jnp.dot(grad_gate_pre, w_gate, preferred_element_type=jnp.float32)
        + jnp.dot(grad_up_pre, w_up, preferred_element_type=jnp.float32)
    ).astype(jnp.bfloat16)
    ff_share = w_gate.shape[0] // copies
    with jax.named_scope("weight_grads"):
        down_term = (
            scale * jnp.einsum("rf,rd->fd", activated, out_grads, preferred_element_type=jnp.float32)
        ).astype(jnp.bfloat16)
        gate_up_pre = jnp.stack(
            [
                grad_gate_pre.reshape(slots, copies, ff_share),
                grad_up_pre.reshape(slots, copies, ff_share),
            ],
            axis=2,
        ).reshape(slots, copies * 2 * ff_share)
        gate_up_term = (
            scale * jnp.einsum("rf,rd->fd", gate_up_pre, in_rows, preferred_element_type=jnp.float32)
        ).astype(jnp.bfloat16)
    down_share = lax.psum_scatter(down_term, "dp", scatter_dimension=0, tiled=True)
    gate_up_share = lax.psum_scatter(gate_up_term, "dp", scatter_dimension=0, tiled=True)
    gate_share = gate_up_share[:ff_share]
    up_share = gate_up_share[ff_share:]
    me = lax.axis_index("expert")
    back_grads = []
    for shift in range(experts):
        chunk = lax.dynamic_slice_in_dim(row_grads, ((me + shift) % experts) * capacity, capacity, 0)
        if shift == experts // 2:
            chunk, gate_share, up_share = lax.optimization_barrier((chunk, gate_share, up_share))
        if shift:
            chunk = lax.ppermute(
                chunk, "expert", [(j, (j + shift) % experts) for j in range(experts)]
            )
        back_grads.append(chunk)
    back_grads = jnp.concatenate(back_grads, axis=0)
    pick_onehot = hit.reshape(top_count * tok_count, slots).astype(jnp.bfloat16)
    with jax.named_scope("combine_rows"):
        picked_out = jnp.dot(
            pick_onehot, back_out.reshape(slots, model_width), preferred_element_type=jnp.float32
        ).reshape(top_count, tok_count, model_width)
        grad_f32 = grad_out.astype(jnp.float32)
        mixed = combine[:, 0:1] * picked_out[0]
        for k in range(1, top_count):
            mixed = mixed + combine[:, k : k + 1] * picked_out[k]
        mixed = mixed.astype(jnp.bfloat16)
        grad_combine = jnp.stack(
            [jnp.sum(grad_f32 * picked_out[k], axis=1) for k in range(top_count)], axis=1
        )
        back_grads, gate_share, up_share, mixed, grad_combine = lax.optimization_barrier(
            (back_grads, gate_share, up_share, mixed, grad_combine)
        )
        shift_target = ((me - expert_ids) % experts) * capacity + target % capacity
        token_onehot = jnp.any(
            shift_target[:, :, None] == slot_iota[None, None, :], axis=1
        ).astype(jnp.bfloat16)
        grad_tokens = jnp.dot(
            token_onehot, back_grads.reshape(slots, model_width), preferred_element_type=jnp.float32
        ).astype(jnp.bfloat16)
    return (mixed, grad_tokens, grad_combine, gate_share[None], up_share[None], down_share[None])


def solution(mesh):
    in_specs = (
        P(("dp", "expert"), None),
        P(("dp", "expert"), None),
        P(("dp", "expert"), None),
        P("expert", None, None),
        P("expert", None, None),
        P("expert", None, None),
        P(("dp", "expert"), None),
    )
    out_specs = (
        P(("dp", "expert"), None),
        P(("dp", "expert"), None),
        P(("dp", "expert"), None),
        P("expert", "dp", None),
        P("expert", "dp", None),
        P("expert", "dp", None),
    )
    return jax.shard_map(
        per_device, mesh=mesh, in_specs=in_specs, out_specs=out_specs, check_vma=False
    )
```
